256 devices in a mesh: lat: 8 (over y, z_lo), lon: 8 (over x, core), dp: 4 (over z_hi).
Axes of the slice: x: 4, y: 4, z: 8 (z_hi: 4, z_lo: 2; z = z_hi * 2 + z_lo), core: 2. Of those that a mesh axis runs over, the one named last changes fastest.
Arguments:
- state_grid: bfloat16 [4, 384, 768, 128], P('dp', ('lat', 'lon')), may hold values from -6 to 6
- cotangent: bfloat16 [4, 384, 768, 128], P('dp', ('lat', 'lon')), may hold values from -6 to 6
- legendre: bfloat16 [384, 384, 384], P(('lat', 'lon')), may hold values from -0.3125 to 0.3125
- wave_ids: int32 [384], replicated, may hold values from 0 to 383, each once
- weights: bfloat16 [384, 2, 4, 1024], P('lat'), may hold values from -0.75 to 0.75
Outputs:
- input_grad: bfloat16 [4, 384, 768, 128], P('dp', ('lat', 'lon'))
- weight_grad: float32 [384, 2, 4, 1024], P('lat')
The draws below stay inside these ranges and needn't reach their ends.
Inputs may be any that keep to these rules, and one draw needn't show every extreme that they name: wave_ids[j] is the wavenumber of slot j; each of 0 to 383 stands in exactly one slot.
All inputs are finite; a program needn't handle non-finite values.
Results may differ from the reference program's by a relative error of at most 0.034.
Values may be sent and summed in bfloat16 or wider, within the bound.
No kernel may reach another device: no remote copies, remote signals or barrier semaphores. Data moves between devices by JAX's collectives and lax.ppermute only.
A program may use at most 128 MiB of HBM per device.

```python
import math
import jax
import jax.numpy as jnp
from jax import lax

NLAT = 384
NLON = 768
MODES = 384
DEGREES = 384
GROUPS = 4
GROUP_WIDTH = 32
CH = 128
BATCH = 4


def steps_of(stream_key, shape, pieces, least, high):
    level, own = 1.0, jax.random.fold_in(stream_key, 6)
    for position, blocks in pieces:
        draws = jnp.exp(jax.random.uniform(jax.random.fold_in(own, position), (blocks,), jnp.float32, least / len(pieces), high / len(pieces)))
        level = level * jnp.repeat(draws, shape[position] // blocks).reshape([-1 if axis == position else 1 for axis in range(len(shape))])
    return level


def normal_values(stream_key, shape, scale, bound, shards=(), held_as=jnp.bfloat16):
    entries = scale * jax.random.normal(stream_key, shape, jnp.float32)
    if shards:
        entries = entries * steps_of(stream_key, shape, shards, -0.22, 0.18)
    return jnp.clip(entries, -bound, bound).astype(held_as)


def setup_inputs(seed: int = 0) -> dict:
    splits = jax.random.split(jax.random.key(seed), 6)
    state_grid = normal_values(splits[0], (BATCH, NLAT, NLON, CH), 1.0, 6.0, ((0, 4), (1, 64)))
    cotangent = normal_values(splits[1], (BATCH, NLAT, NLON, CH), 1.0, 6.0, ((0, 4), (1, 64)))
    legendre = normal_values(splits[2], (MODES, NLAT, DEGREES), NLAT ** -0.5, 0.3125, ((0, 64),))
    wave_ids = jax.random.permutation(splits[3], MODES).astype(jnp.int32)
    weights = normal_values(splits[4], (DEGREES, 2, GROUPS, GROUP_WIDTH * GROUP_WIDTH), (2 * GROUP_WIDTH) ** -0.5, 0.75, ((0, 8),))
    return dict(state_grid=state_grid, cotangent=cotangent, legendre=legendre, wave_ids=wave_ids, weights=weights)


def build_tables(wave_ids):
    columns = jnp.arange(NLON, dtype=jnp.int32)
    phase_int = wave_ids[:, None] * columns[None, :] % NLON
    angles = phase_int.astype(jnp.float32) * jnp.float32(2.0 * math.pi / NLON)
    factor = jnp.float32(1.0 / math.sqrt(NLON))
    paired = jnp.stack([jnp.cos(angles) * factor, -jnp.sin(angles) * factor], axis=1)
    forward_table = paired.reshape(2 * wave_ids.shape[0], NLON)
    doubling = jnp.where(wave_ids == 0, 1.0, 2.0).astype(jnp.float32)
    inverse_table = forward_table * jnp.repeat(doubling, 2)[:, None]
    return (forward_table.astype(jnp.bfloat16), inverse_table.astype(jnp.bfloat16))

def build_kernel(weights):
    degree_count = weights.shape[0]
    real_part = weights[:, 0].reshape(degree_count, GROUPS, GROUP_WIDTH, GROUP_WIDTH)
    imag_part = weights[:, 1].reshape(degree_count, GROUPS, GROUP_WIDTH, GROUP_WIDTH)
    upper_rows = jnp.stack([real_part, imag_part], axis=3)
    lower_rows = jnp.stack([-imag_part, real_part], axis=3)
    return jnp.stack([upper_rows, lower_rows], axis=2)

def gelu_slope(branch):
    normal_cdf = 0.5 * (1.0 + lax.erf(branch * (1.0 / math.sqrt(2.0))))
    density = jnp.exp(-0.5 * branch * branch) * (1.0 / math.sqrt(2.0 * math.pi))
    return normal_cdf + branch * density

def analyze(source, twiddle, masked_wide):
    spectra = jnp.einsum('anc,kn->akc', source.astype(jnp.float32), twiddle.astype(jnp.float32)).astype(jnp.bfloat16)
    spectra = spectra.reshape(NLAT, MODES, 2 * CH).astype(jnp.float32)
    coef_out = jnp.einsum('jal,ajc->ljc', masked_wide, spectra).astype(jnp.bfloat16)
    return coef_out.reshape(DEGREES, MODES, 2, GROUPS, GROUP_WIDTH)

def synthesize(coef_in, twiddle, masked_wide):
    flat_coef = coef_in.reshape(DEGREES, MODES, 2 * CH).astype(jnp.float32)
    spectra = jnp.einsum('jal,ljc->ajc', masked_wide, flat_coef).astype(jnp.bfloat16)
    spectra = spectra.reshape(NLAT, 2 * MODES, CH).astype(jnp.float32)
    return jnp.einsum('akc,kn->anc', spectra, twiddle.astype(jnp.float32))

def reference(state_grid, cotangent, legendre, wave_ids, weights):
    forward_table, inverse_table = build_tables(wave_ids)
    degree_ids = jnp.arange(DEGREES, dtype=jnp.int32)
    masked = jnp.where(degree_ids[None, None, :] >= wave_ids[:, None, None], legendre, jnp.zeros((), legendre.dtype))
    masked_wide = masked.astype(jnp.float32)
    kernel = build_kernel(weights).astype(jnp.float32)

    def one_sample(running, sample_pair):
        source, cot_sample = sample_pair
        coef_fwd = analyze(source, forward_table, masked_wide)
        mixed = jnp.einsum('lmpgi,lgpiqo->lmqgo', coef_fwd.astype(jnp.float32), kernel).astype(jnp.bfloat16)
        branch = synthesize(mixed, inverse_table, masked_wide)
        pulled = (cot_sample.astype(jnp.float32) * gelu_slope(branch)).astype(jnp.bfloat16)
        back_coef = analyze(pulled, inverse_table, masked_wide)
        running = running + jnp.einsum('lmpgi,lmqgo->lgpiqo', coef_fwd.astype(jnp.float32), back_coef.astype(jnp.float32))
        demixed = jnp.einsum('lmqgo,lgpiqo->lmpgi', back_coef.astype(jnp.float32), kernel).astype(jnp.bfloat16)
        input_grad = (cot_sample.astype(jnp.float32) + synthesize(demixed, forward_table, masked_wide)).astype(jnp.bfloat16)
        return (running, input_grad)
    start_sums = jnp.zeros((DEGREES, GROUPS, 2, GROUP_WIDTH, 2, GROUP_WIDTH), jnp.float32)
    outer_sums, input_grad = lax.scan(one_sample, start_sums, (state_grid, cotangent))
    real_grad = outer_sums[:, :, 0, :, 0, :] + outer_sums[:, :, 1, :, 1, :]
    imag_grad = outer_sums[:, :, 0, :, 1, :] - outer_sums[:, :, 1, :, 0, :]
    weight_grad = jnp.stack([real_grad, imag_grad], axis=1).reshape(DEGREES, 2, GROUPS, GROUP_WIDTH * GROUP_WIDTH)
    return (input_grad, weight_grad)
```

```python
import math

import jax
import jax.numpy as jnp
from jax import lax
from jax.sharding import PartitionSpec as P

NLON = 768
GROUPS = 4
GROUP_WIDTH = 32


def build_tables(wave_ids):
    columns = jnp.arange(NLON, dtype=jnp.int32)
    phase_int = wave_ids[:, None] * columns[None, :] % NLON
    angles = phase_int.astype(jnp.float32) * jnp.float32(2.0 * math.pi / NLON)
    factor = jnp.float32(1.0 / math.sqrt(NLON))
    paired = jnp.stack([jnp.cos(angles) * factor, -jnp.sin(angles) * factor], axis=1)
    forward_table = paired.reshape(2 * wave_ids.shape[0], NLON)
    doubling = jnp.where(wave_ids == 0, 1.0, 2.0).astype(jnp.float32)
    inverse_table = forward_table * jnp.repeat(doubling, 2)[:, None]
    return (forward_table.astype(jnp.bfloat16), inverse_table.astype(jnp.bfloat16))


def build_kernel(weights):
    degree_count = weights.shape[0]
    real_part = weights[:, 0].reshape(degree_count, GROUPS, GROUP_WIDTH, GROUP_WIDTH)
    imag_part = weights[:, 1].reshape(degree_count, GROUPS, GROUP_WIDTH, GROUP_WIDTH)
    upper_rows = jnp.stack([real_part, imag_part], axis=3)
    lower_rows = jnp.stack([-imag_part, real_part], axis=3)
    return jnp.stack([upper_rows, lower_rows], axis=2)


def gelu_slope(branch):
    normal_cdf = 0.5 * (1.0 + lax.erf(branch * (1.0 / math.sqrt(2.0))))
    density = jnp.exp(-0.5 * branch * branch) * (1.0 / math.sqrt(2.0 * math.pi))
    return normal_cdf + branch * density


def reduce_over(values, axes):
    count = 1
    for name in axes:
        count *= lax.axis_size(name)
    chunks = values.reshape(count, -1)
    scattered = lax.all_to_all(chunks, axes, split_axis=0, concat_axis=0, tiled=True)
    reduced = jnp.sum(scattered.astype(jnp.float32), axis=0).astype(values.dtype)
    tiled = jnp.broadcast_to(reduced[None], (count, reduced.shape[0]))
    gathered = lax.all_to_all(tiled, axes, split_axis=0, concat_axis=0, tiled=True)
    return gathered.reshape(values.shape)


def shards(state_grid, cotangent, legendre, wave_ids, weights):
    lat_count = lax.axis_size("lat")
    lon_count = lax.axis_size("lon")
    samples, rows_dev, lon_cells, channels = state_grid.shape
    slot_count, lat_cells, degree_count = legendre.shape
    slot_reals = 2 * slot_count
    first_slot = (lax.axis_index("lat") * lon_count + lax.axis_index("lon")) * slot_count
    held_waves = lax.dynamic_slice_in_dim(wave_ids, first_slot, slot_count)
    degree_ids = jnp.arange(degree_count, dtype=jnp.int32)
    masked = jnp.where(
        degree_ids[None, None, :] >= held_waves[:, None, None],
        legendre,
        jnp.zeros((), legendre.dtype),
    )
    slot_order = wave_ids.reshape(lat_count, lon_count, slot_count).transpose(1, 0, 2).reshape(-1)
    forward_table, inverse_table = build_tables(slot_order)
    kernel = build_kernel(weights)

    def analyze(source, twiddle):
        spectra = jnp.einsum(
            "srnc,kn->srkc", source, twiddle, preferred_element_type=jnp.float32
        ).astype(jnp.bfloat16)
        gathered = lax.all_to_all(
            lax.all_to_all(spectra, "lon", split_axis=2, concat_axis=1, tiled=True),
            "lat",
            split_axis=2,
            concat_axis=1,
            tiled=True,
        )
        blocks = gathered.reshape(samples, lat_cells, slot_count, 2 * channels)
        spectral = jnp.einsum("samc,mal->slmc", blocks, masked, preferred_element_type=jnp.float32)
        spectral = spectral.astype(jnp.bfloat16).reshape(
            samples, degree_count, slot_reals, channels
        )
        return lax.all_to_all(spectral, "lat", split_axis=1, concat_axis=2, tiled=True)

    def synthesize(spectral, twiddle):
        joined = lax.all_to_all(spectral, "lat", split_axis=2, concat_axis=1, tiled=True)
        blocks = joined.reshape(samples, degree_count, slot_count, 2 * channels)
        spectra = jnp.einsum(
            "slmc,mal->samc", blocks, masked, preferred_element_type=jnp.float32
        ).astype(jnp.bfloat16)
        spectra = spectra.reshape(samples, lat_cells, slot_reals, channels)
        pencil = lax.all_to_all(
            lax.all_to_all(spectra, "lat", split_axis=1, concat_axis=2, tiled=True),
            "lon",
            split_axis=1,
            concat_axis=2,
            tiled=True,
        )
        return jnp.einsum("srkc,kn->srnc", pencil, twiddle, preferred_element_type=jnp.float32)

    def split_groups(spectral):
        return spectral.reshape(samples, spectral.shape[1], -1, 2, GROUPS, GROUP_WIDTH)

    coef_fwd = analyze(state_grid, forward_table)
    coef_six = split_groups(coef_fwd)
    mixed_coef = jnp.einsum(
        "slmpgi,lgpiqo->slmqgo", coef_six, kernel, preferred_element_type=jnp.float32
    ).astype(jnp.bfloat16)
    branch = synthesize(mixed_coef.reshape(coef_fwd.shape), inverse_table)
    pulled = (cotangent.astype(jnp.float32) * gelu_slope(branch)).astype(jnp.bfloat16)
    back_coef = analyze(pulled, inverse_table)
    back_six = split_groups(back_coef)
    outer_sums = jnp.einsum(
        "slmpgi,slmqgo->lgpiqo", coef_six, back_six, preferred_element_type=jnp.float32
    )
    real_grad = outer_sums[:, :, 0, :, 0, :] + outer_sums[:, :, 1, :, 1, :]
    imag_grad = outer_sums[:, :, 0, :, 1, :] - outer_sums[:, :, 1, :, 0, :]
    local_grad = jnp.stack([real_grad, imag_grad], axis=1).reshape(weights.shape)
    weight_grad = reduce_over(local_grad.astype(jnp.bfloat16), ("lon", "dp")).astype(jnp.float32)
    demixed = jnp.einsum(
        "slmqgo,lgpiqo->slmpgi", back_six, kernel, preferred_element_type=jnp.float32
    ).astype(jnp.bfloat16)
    returned = synthesize(demixed.reshape(back_coef.shape), forward_table)
    input_grad = (cotangent.astype(jnp.float32) + returned).astype(jnp.bfloat16)
    return (input_grad, weight_grad)


def solution(mesh):
    return jax.shard_map(
        shards,
        mesh=mesh,
        in_specs=(
            P("dp", ("lat", "lon"), None, None),
            P("dp", ("lat", "lon"), None, None),
            P(("lat", "lon"), None, None),
            P(),
            P("lat", None, None, None),
        ),
        out_specs=(P("dp", ("lat", "lon"), None, None), P("lat", None, None, None)),
        check_vma=False,
    )
```

```python
import math

import jax
import jax.numpy as jnp
from jax import lax
from jax.sharding import PartitionSpec as P

NLON = 768
GROUPS = 4
GROUP_WIDTH = 32


def build_tables(wave_ids):
    columns = jnp.arange(NLON, dtype=jnp.int32)
    phase_int = wave_ids[:, None] * columns[None, :] % NLON
    angles = phase_int.astype(jnp.float32) * jnp.float32(2.0 * math.pi / NLON)
    factor = jnp.float32(1.0 / math.sqrt(NLON))
    paired = jnp.stack([jnp.cos(angles) * factor, -jnp.sin(angles) * factor], axis=1)
    forward_table = paired.reshape(2 * wave_ids.shape[0], NLON)
    doubling = jnp.where(wave_ids == 0, 1.0, 2.0).astype(jnp.float32)
    inverse_table = forward_table * jnp.repeat(doubling, 2)[:, None]
    return (forward_table.astype(jnp.bfloat16), inverse_table.astype(jnp.bfloat16))


def build_kernel(weights):
    degree_count = weights.shape[0]
    real_part = weights[:, 0].reshape(degree_count, GROUPS, GROUP_WIDTH, GROUP_WIDTH)
    imag_part = weights[:, 1].reshape(degree_count, GROUPS, GROUP_WIDTH, GROUP_WIDTH)
    upper_rows = jnp.stack([real_part, imag_part], axis=3)
    lower_rows = jnp.stack([-imag_part, real_part], axis=3)
    return jnp.stack([upper_rows, lower_rows], axis=2)


def gelu_slope(branch):
    normal_cdf = 0.5 * (1.0 + lax.erf(branch * (1.0 / math.sqrt(2.0))))
    density = jnp.exp(-0.5 * branch * branch) * (1.0 / math.sqrt(2.0 * math.pi))
    return normal_cdf + branch * density


def reduce_over(values, axes):
    count = 1
    for name in axes:
        count *= lax.axis_size(name)
    chunks = values.reshape(count, -1)
    scattered = lax.all_to_all(chunks, axes, split_axis=0, concat_axis=0, tiled=True)
    reduced = jnp.sum(scattered.astype(jnp.float32), axis=0).astype(values.dtype)
    tiled = jnp.broadcast_to(reduced[None], (count, reduced.shape[0]))
    gathered = lax.all_to_all(tiled, axes, split_axis=0, concat_axis=0, tiled=True)
    return gathered.reshape(values.shape)


def shards(state_grid, cotangent, legendre, wave_ids, weights):
    lat_count = lax.axis_size("lat")
    lon_count = lax.axis_size("lon")
    samples, rows_dev, lon_cells, channels = state_grid.shape
    slot_count, lat_cells, degree_count = legendre.shape
    slot_reals = 2 * slot_count
    first_slot = (lax.axis_index("lat") * lon_count + lax.axis_index("lon")) * slot_count
    held_waves = lax.dynamic_slice_in_dim(wave_ids, first_slot, slot_count)
    degree_ids = jnp.arange(degree_count, dtype=jnp.int32)
    masked = jnp.where(
        degree_ids[None, None, :] >= held_waves[:, None, None],
        legendre,
        jnp.zeros((), legendre.dtype),
    )
    forward_table, inverse_table = build_tables(wave_ids)
    kernel = build_kernel(weights)

    def analyze(source, twiddle):
        spectra = jnp.einsum(
            "srnc,kn->srkc", source, twiddle, preferred_element_type=jnp.float32
        ).astype(jnp.bfloat16)
        gathered = lax.all_to_all(spectra, ("lat", "lon"), split_axis=2, concat_axis=1, tiled=True)
        blocks = gathered.reshape(samples, lat_cells, slot_count, 2 * channels)
        spectral = jnp.einsum("samc,mal->slmc", blocks, masked, preferred_element_type=jnp.float32)
        spectral = spectral.astype(jnp.bfloat16).reshape(
            samples, degree_count, slot_reals, channels
        )
        return lax.all_to_all(spectral, "lat", split_axis=1, concat_axis=2, tiled=True)

    def synthesize(spectral, twiddle):
        joined = lax.all_to_all(spectral, "lat", split_axis=2, concat_axis=1, tiled=True)
        blocks = joined.reshape(samples, degree_count, slot_count, 2 * channels)
        spectra = jnp.einsum(
            "slmc,mal->samc", blocks, masked, preferred_element_type=jnp.float32
        ).astype(jnp.bfloat16)
        spectra = spectra.reshape(samples, lat_cells, slot_reals, channels)
        pencil = lax.all_to_all(spectra, ("lat", "lon"), split_axis=1, concat_axis=2, tiled=True)
        return jnp.einsum("srkc,kn->srnc", pencil, twiddle, preferred_element_type=jnp.float32)

    def split_groups(spectral):
        return spectral.reshape(samples, spectral.shape[1], -1, 2, GROUPS, GROUP_WIDTH)

    coef_fwd = analyze(state_grid, forward_table)
    coef_six = split_groups(coef_fwd)
    mixed_coef = jnp.einsum(
        "slmpgi,lgpiqo->slmqgo", coef_six, kernel, preferred_element_type=jnp.float32
    ).astype(jnp.bfloat16)
    branch = synthesize(mixed_coef.reshape(coef_fwd.shape), inverse_table)
    pulled = (cotangent.astype(jnp.float32) * gelu_slope(branch)).astype(jnp.bfloat16)
    back_coef = analyze(pulled, inverse_table)
    back_six = split_groups(back_coef)
    outer_sums = jnp.einsum(
        "slmpgi,slmqgo->lgpiqo", coef_six, back_six, preferred_element_type=jnp.float32
    )
    real_grad = outer_sums[:, :, 0, :, 0, :] + outer_sums[:, :, 1, :, 1, :]
    imag_grad = outer_sums[:, :, 0, :, 1, :] - outer_sums[:, :, 1, :, 0, :]
    local_grad = jnp.stack([real_grad, imag_grad], axis=1).reshape(weights.shape)
    weight_grad = reduce_over(local_grad.astype(jnp.bfloat16), ("lon", "dp")).astype(jnp.float32)
    demixed = jnp.einsum(
        "slmqgo,lgpiqo->slmpgi", back_six, kernel, preferred_element_type=jnp.float32
    ).astype(jnp.bfloat16)
    returned = synthesize(demixed.reshape(back_coef.shape), forward_table)
    input_grad = (cotangent.astype(jnp.float32) + returned).astype(jnp.bfloat16)
    return (input_grad, weight_grad)


def solution(mesh):
    return jax.shard_map(
        shards,
        mesh=mesh,
        in_specs=(
            P("dp", ("lat", "lon"), None, None),
            P("dp", ("lat", "lon"), None, None),
            P(("lat", "lon"), None, None),
            P(),
            P("lat", None, None, None),
        ),
        out_specs=(P("dp", ("lat", "lon"), None, None), P("lat", None, None, None)),
        check_vma=False,
    )
```

```python
import math

import jax
import jax.numpy as jnp
from jax import lax
from jax.sharding import PartitionSpec as P

NLON = 768
GROUPS = 4
GROUP_WIDTH = 32


def build_tables(wave_ids):
    columns = jnp.arange(NLON, dtype=jnp.int32)
    phase_int = wave_ids[:, None] * columns[None, :] % NLON
    angles = phase_int.astype(jnp.float32) * jnp.float32(2.0 * math.pi / NLON)
    factor = jnp.float32(1.0 / math.sqrt(NLON))
    paired = jnp.stack([jnp.cos(angles) * factor, -jnp.sin(angles) * factor], axis=1)
    forward_table = paired.reshape(2 * wave_ids.shape[0], NLON)
    doubling = jnp.where(wave_ids == 0, 1.0, 2.0).astype(jnp.float32)
    inverse_table = forward_table * jnp.repeat(doubling, 2)[:, None]
    return (forward_table.astype(jnp.bfloat16), inverse_table.astype(jnp.bfloat16))


def block_diagonal(weights):
    degree_count = weights.shape[0]
    width = GROUPS * GROUP_WIDTH
    parts = weights.reshape(degree_count, 2, width, GROUP_WIDTH)
    spread = jnp.tile(parts, (1, 1, 1, GROUPS))
    rows = lax.broadcasted_iota(jnp.int32, (width, width), 0) // GROUP_WIDTH
    cols = lax.broadcasted_iota(jnp.int32, (width, width), 1) // GROUP_WIDTH
    blocks = jnp.where(rows == cols, spread, jnp.zeros((), weights.dtype))
    return blocks[:, 0], blocks[:, 1]


def build_kernel(weights):
    degree_count = weights.shape[0]
    real_part = weights[:, 0].reshape(degree_count, GROUPS, GROUP_WIDTH, GROUP_WIDTH)
    imag_part = weights[:, 1].reshape(degree_count, GROUPS, GROUP_WIDTH, GROUP_WIDTH)
    upper_rows = jnp.stack([real_part, imag_part], axis=3)
    lower_rows = jnp.stack([-imag_part, real_part], axis=3)
    return jnp.stack([upper_rows, lower_rows], axis=2)


def gelu_slope(branch):
    normal_cdf = 0.5 * (1.0 + lax.erf(branch * (1.0 / math.sqrt(2.0))))
    density = jnp.exp(-0.5 * branch * branch) * (1.0 / math.sqrt(2.0 * math.pi))
    return normal_cdf + branch * density


def reduce_over(values, axes):
    count = 1
    for name in axes:
        count *= lax.axis_size(name)
    chunks = values.reshape(count, -1)
    scattered = lax.all_to_all(chunks, axes, split_axis=0, concat_axis=0, tiled=True)
    reduced = jnp.sum(scattered.astype(jnp.float32), axis=0).astype(values.dtype)
    tiled = jnp.broadcast_to(reduced[None], (count, reduced.shape[0]))
    gathered = lax.all_to_all(tiled, axes, split_axis=0, concat_axis=0, tiled=True)
    return gathered.reshape(values.shape)


def shards(state_grid, cotangent, legendre, wave_ids, weights):
    lat_count = lax.axis_size("lat")
    lon_count = lax.axis_size("lon")
    samples, rows_dev, lon_cells, channels = state_grid.shape
    slot_count, lat_cells, degree_count = legendre.shape
    slot_reals = 2 * slot_count
    first_slot = (lax.axis_index("lat") * lon_count + lax.axis_index("lon")) * slot_count
    held_waves = lax.dynamic_slice_in_dim(wave_ids, first_slot, slot_count)
    degree_ids = jnp.arange(degree_count, dtype=jnp.int32)
    masked = jnp.where(
        degree_ids[None, None, :] >= held_waves[:, None, None],
        legendre,
        jnp.zeros((), legendre.dtype),
    )
    forward_table, inverse_table = build_tables(wave_ids)

    def analyze(source, twiddle):
        spectra = jnp.einsum(
            "srnc,kn->srkc", source, twiddle, preferred_element_type=jnp.float32
        ).astype(jnp.bfloat16)
        gathered = lax.all_to_all(spectra, ("lat", "lon"), split_axis=2, concat_axis=1, tiled=True)
        blocks = gathered.reshape(samples, lat_cells, slot_count, 2 * channels)
        spectral = jnp.einsum("samc,mal->slmc", blocks, masked, preferred_element_type=jnp.float32)
        spectral = spectral.astype(jnp.bfloat16).reshape(
            samples, degree_count, slot_reals, channels
        )
        return lax.all_to_all(spectral, "lat", split_axis=1, concat_axis=2, tiled=True)

    def synthesize(spectral, twiddle):
        joined = lax.all_to_all(spectral, "lat", split_axis=2, concat_axis=1, tiled=True)
        blocks = joined.reshape(samples, degree_count, slot_count, 2 * channels)
        spectra = jnp.einsum(
            "slmc,mal->samc", blocks, masked, preferred_element_type=jnp.float32
        ).astype(jnp.bfloat16)
        spectra = spectra.reshape(samples, lat_cells, slot_reals, channels)
        pencil = lax.all_to_all(spectra, ("lat", "lon"), split_axis=1, concat_axis=2, tiled=True)
        return jnp.einsum("srkc,kn->srnc", pencil, twiddle, preferred_element_type=jnp.float32)

    coef_fwd = analyze(state_grid, forward_table)
    coef_rows = coef_fwd[0]
    real_bd, imag_bd = block_diagonal(weights)
    row_ids = lax.broadcasted_iota(jnp.int32, coef_rows.shape, 1)
    even_rows = row_ids % 2 == 0

    def rolled(values, shift):
        return jnp.roll(values, shift, axis=1)

    real_prod = jnp.einsum("lrc,lcd->lrd", coef_rows, real_bd, preferred_element_type=jnp.float32)
    imag_prod = jnp.einsum("lrc,lcd->lrd", coef_rows, imag_bd, preferred_element_type=jnp.float32)
    mixed_rows = jnp.where(
        even_rows, real_prod - rolled(imag_prod, -1), real_prod + rolled(imag_prod, 1)
    ).astype(jnp.bfloat16)
    branch = synthesize(mixed_rows[None], inverse_table)
    pulled = (cotangent.astype(jnp.float32) * gelu_slope(branch)).astype(jnp.bfloat16)
    back_coef = analyze(pulled, inverse_table)
    back_rows = back_coef[0]
    swapped = jnp.where(even_rows, rolled(back_rows, -1), -rolled(back_rows, 1))
    grad_full = jnp.einsum(
        "lrc,lrd->lcd",
        coef_rows,
        jnp.concatenate([back_rows, swapped], axis=2),
        preferred_element_type=jnp.float32,
    ).reshape(weights.shape[0], GROUPS, GROUP_WIDTH, 2, GROUPS, GROUP_WIDTH)
    same_group = jnp.eye(GROUPS, dtype=jnp.float32)[:, None, None, :, None]
    local_grad = jnp.sum(grad_full * same_group, axis=4).transpose(0, 3, 1, 2, 4)
    local_grad = local_grad.reshape(weights.shape)
    weight_grad = reduce_over(local_grad.astype(jnp.bfloat16), ("lon", "dp")).astype(jnp.float32)
    real_back = jnp.einsum("lrd,lcd->lrc", back_rows, real_bd, preferred_element_type=jnp.float32)
    imag_back = jnp.einsum("lrd,lcd->lrc", back_rows, imag_bd, preferred_element_type=jnp.float32)
    demixed_rows = jnp.where(
        even_rows, real_back + rolled(imag_back, -1), real_back - rolled(imag_back, 1)
    ).astype(jnp.bfloat16)
    returned = synthesize(demixed_rows[None], forward_table)
    input_grad = (cotangent.astype(jnp.float32) + returned).astype(jnp.bfloat16)
    return (input_grad, weight_grad)


def solution(mesh):
    return jax.shard_map(
        shards,
        mesh=mesh,
        in_specs=(
            P("dp", ("lat", "lon"), None, None),
            P("dp", ("lat", "lon"), None, None),
            P(("lat", "lon"), None, None),
            P(),
            P("lat", None, None, None),
        ),
        out_specs=(P("dp", ("lat", "lon"), None, None), P("lat", None, None, None)),
        check_vma=False,
    )
```

```python
import math

import jax
import jax.numpy as jnp
from jax import lax
from jax.sharding import PartitionSpec as P

NLON = 768
GROUPS = 4
GROUP_WIDTH = 32


def build_tables(wave_ids):
    columns = jnp.arange(NLON, dtype=jnp.int32)
    phase_int = wave_ids[:, None] * columns[None, :] % NLON
    angles = phase_int.astype(jnp.float32) * jnp.float32(2.0 * math.pi / NLON)
    factor = jnp.float32(1.0 / math.sqrt(NLON))
    paired = jnp.stack([jnp.cos(angles) * factor, -jnp.sin(angles) * factor], axis=1)
    forward_table = paired.reshape(2 * wave_ids.shape[0], NLON)
    doubling = jnp.where(wave_ids == 0, 1.0, 2.0).astype(jnp.float32)
    inverse_table = forward_table * jnp.repeat(doubling, 2)[:, None]
    return (forward_table.astype(jnp.bfloat16), inverse_table.astype(jnp.bfloat16))


def block_diagonal(weights):
    degree_count = weights.shape[0]
    width = GROUPS * GROUP_WIDTH
    parts = weights.reshape(degree_count, 2, width, GROUP_WIDTH)
    spread = jnp.tile(parts, (1, 1, 1, GROUPS))
    rows = lax.broadcasted_iota(jnp.int32, (width, width), 0) // GROUP_WIDTH
    cols = lax.broadcasted_iota(jnp.int32, (width, width), 1) // GROUP_WIDTH
    blocks = jnp.where(rows == cols, spread, jnp.zeros((), weights.dtype))
    return blocks[:, 0], blocks[:, 1]


def build_kernel(weights):
    degree_count = weights.shape[0]
    real_part = weights[:, 0].reshape(degree_count, GROUPS, GROUP_WIDTH, GROUP_WIDTH)
    imag_part = weights[:, 1].reshape(degree_count, GROUPS, GROUP_WIDTH, GROUP_WIDTH)
    upper_rows = jnp.stack([real_part, imag_part], axis=3)
    lower_rows = jnp.stack([-imag_part, real_part], axis=3)
    return jnp.stack([upper_rows, lower_rows], axis=2)


def gelu_slope(branch):
    normal_cdf = 0.5 * (1.0 + lax.erf(branch * (1.0 / math.sqrt(2.0))))
    density = jnp.exp(-0.5 * branch * branch) * (1.0 / math.sqrt(2.0 * math.pi))
    return normal_cdf + branch * density


def reduce_over(values, axes):
    count = 1
    for name in axes:
        count *= lax.axis_size(name)
    rows = values.reshape(-1, values.shape[-1])
    chunks = rows.reshape(count, rows.shape[0] // count, rows.shape[1])
    scattered = lax.all_to_all(chunks, axes, split_axis=0, concat_axis=0, tiled=True)
    reduced = jnp.sum(scattered.astype(jnp.float32), axis=0).astype(values.dtype)
    tiled = jnp.broadcast_to(reduced[None], (count,) + reduced.shape)
    gathered = lax.all_to_all(tiled, axes, split_axis=0, concat_axis=0, tiled=True)
    return gathered.reshape(values.shape)


def shards(state_grid, cotangent, legendre, wave_ids, weights):
    lat_count = lax.axis_size("lat")
    lon_count = lax.axis_size("lon")
    samples, rows_dev, lon_cells, channels = state_grid.shape
    slot_count, lat_cells, degree_count = legendre.shape
    slot_reals = 2 * slot_count
    first_slot = (lax.axis_index("lat") * lon_count + lax.axis_index("lon")) * slot_count
    held_waves = lax.dynamic_slice_in_dim(wave_ids, first_slot, slot_count)
    degree_ids = jnp.arange(degree_count, dtype=jnp.int32)
    masked = jnp.where(
        degree_ids[None, None, :] >= held_waves[:, None, None],
        legendre,
        jnp.zeros((), legendre.dtype),
    )
    forward_table, inverse_table = build_tables(wave_ids)

    def analyze(source, twiddle):
        spectra = jnp.einsum(
            "srnc,kn->srkc", source, twiddle, preferred_element_type=jnp.float32
        ).astype(jnp.bfloat16)
        gathered = lax.all_to_all(spectra, ("lat", "lon"), split_axis=2, concat_axis=1, tiled=True)
        blocks = gathered.reshape(samples, lat_cells, slot_count, 2 * channels)
        spectral = jnp.einsum("samc,mal->slmc", blocks, masked, preferred_element_type=jnp.float32)
        spectral = spectral.astype(jnp.bfloat16).reshape(
            samples, degree_count, slot_reals, channels
        )
        return lax.all_to_all(spectral, "lat", split_axis=1, concat_axis=2, tiled=True)

    def synthesize(spectral, twiddle):
        joined = lax.all_to_all(spectral, "lat", split_axis=2, concat_axis=1, tiled=True)
        blocks = joined.reshape(samples, degree_count, slot_count, 2 * channels)
        spectra = jnp.einsum(
            "slmc,mal->samc", blocks, masked, preferred_element_type=jnp.float32
        ).astype(jnp.bfloat16)
        spectra = spectra.reshape(samples, lat_cells, slot_reals, channels)
        pencil = lax.all_to_all(spectra, ("lat", "lon"), split_axis=1, concat_axis=2, tiled=True)
        return jnp.einsum("srkc,kn->srnc", pencil, twiddle, preferred_element_type=jnp.float32)

    coef_fwd = analyze(state_grid, forward_table)
    coef_rows = coef_fwd[0]
    real_bd, imag_bd = block_diagonal(weights)
    row_ids = lax.broadcasted_iota(jnp.int32, coef_rows.shape, 1)
    even_rows = row_ids % 2 == 0

    def rolled(values, shift):
        return jnp.roll(values, shift, axis=1)

    real_prod = jnp.einsum("lrc,lcd->lrd", coef_rows, real_bd, preferred_element_type=jnp.float32)
    imag_prod = jnp.einsum("lrc,lcd->lrd", coef_rows, imag_bd, preferred_element_type=jnp.float32)
    mixed_rows = jnp.where(
        even_rows, real_prod - rolled(imag_prod, -1), real_prod + rolled(imag_prod, 1)
    ).astype(jnp.bfloat16)
    branch = synthesize(mixed_rows[None], inverse_table)
    pulled = (cotangent.astype(jnp.float32) * gelu_slope(branch)).astype(jnp.bfloat16)
    back_coef = analyze(pulled, inverse_table)
    back_rows = back_coef[0]
    swapped = jnp.where(even_rows, rolled(back_rows, -1), -rolled(back_rows, 1))
    grad_full = jnp.einsum(
        "lrc,lrd->lcd",
        coef_rows,
        jnp.concatenate([back_rows, swapped], axis=2),
        preferred_element_type=jnp.float32,
    )
    width = GROUPS * GROUP_WIDTH
    local_grad = jnp.stack(
        [
            jnp.stack(
                [
                    grad_full[
                        :,
                        g * GROUP_WIDTH : (g + 1) * GROUP_WIDTH,
                        t * width + g * GROUP_WIDTH : t * width + (g + 1) * GROUP_WIDTH,
                    ]
                    for g in range(GROUPS)
                ],
                axis=1,
            )
            for t in range(2)
        ],
        axis=1,
    ).reshape(weights.shape)
    weight_grad = reduce_over(local_grad.astype(jnp.bfloat16), ("lon", "dp")).astype(jnp.float32)
    real_back = jnp.einsum("lrd,lcd->lrc", back_rows, real_bd, preferred_element_type=jnp.float32)
    imag_back = jnp.einsum("lrd,lcd->lrc", back_rows, imag_bd, preferred_element_type=jnp.float32)
    demixed_rows = jnp.where(
        even_rows, real_back + rolled(imag_back, -1), real_back - rolled(imag_back, 1)
    ).astype(jnp.bfloat16)
    returned = synthesize(demixed_rows[None], forward_table)
    input_grad = (cotangent.astype(jnp.float32) + returned).astype(jnp.bfloat16)
    return (input_grad, weight_grad)


def solution(mesh):
    return jax.shard_map(
        shards,
        mesh=mesh,
        in_specs=(
            P("dp", ("lat", "lon"), None, None),
            P("dp", ("lat", "lon"), None, None),
            P(("lat", "lon"), None, None),
            P(),
            P("lat", None, None, None),
        ),
        out_specs=(P("dp", ("lat", "lon"), None, None), P("lat", None, None, None)),
        check_vma=False,
    )
```

```python
import math

import jax
import jax.numpy as jnp
from jax import lax
from jax.sharding import PartitionSpec as P

NLON = 768
GROUPS = 4
GROUP_WIDTH = 32


def build_tables(wave_ids):
    columns = jnp.arange(NLON, dtype=jnp.int32)
    phase_int = wave_ids[:, None] * columns[None, :] % NLON
    angles = phase_int.astype(jnp.float32) * jnp.float32(2.0 * math.pi / NLON)
    factor = jnp.float32(1.0 / math.sqrt(NLON))
    paired = jnp.stack([jnp.cos(angles) * factor, -jnp.sin(angles) * factor], axis=1)
    forward_table = paired.reshape(2 * wave_ids.shape[0], NLON)
    doubling = jnp.where(wave_ids == 0, 1.0, 2.0).astype(jnp.float32)
    inverse_table = forward_table * jnp.repeat(doubling, 2)[:, None]
    return (forward_table.astype(jnp.bfloat16), inverse_table.astype(jnp.bfloat16))


def block_diagonal(weights):
    degree_count = weights.shape[0]
    width = GROUPS * GROUP_WIDTH
    parts = weights.reshape(degree_count, 2, width, GROUP_WIDTH)
    spread = jnp.tile(parts, (1, 1, 1, GROUPS))
    rows = lax.broadcasted_iota(jnp.int32, (width, width), 0) // GROUP_WIDTH
    cols = lax.broadcasted_iota(jnp.int32, (width, width), 1) // GROUP_WIDTH
    blocks = jnp.where(rows == cols, spread, jnp.zeros((), weights.dtype))
    return blocks[:, 0], blocks[:, 1]


def build_kernel(weights):
    degree_count = weights.shape[0]
    real_part = weights[:, 0].reshape(degree_count, GROUPS, GROUP_WIDTH, GROUP_WIDTH)
    imag_part = weights[:, 1].reshape(degree_count, GROUPS, GROUP_WIDTH, GROUP_WIDTH)
    upper_rows = jnp.stack([real_part, imag_part], axis=3)
    lower_rows = jnp.stack([-imag_part, real_part], axis=3)
    return jnp.stack([upper_rows, lower_rows], axis=2)


def gelu_slope(branch):
    normal_cdf = 0.5 * (1.0 + lax.erf(branch * (1.0 / math.sqrt(2.0))))
    density = jnp.exp(-0.5 * branch * branch) * (1.0 / math.sqrt(2.0 * math.pi))
    return normal_cdf + branch * density


def reduce_over(values, axes):
    count = 1
    for name in axes:
        count *= lax.axis_size(name)
    rows = values.reshape(-1, values.shape[-1])
    chunks = rows.reshape(count, rows.shape[0] // count, rows.shape[1])
    scattered = lax.all_to_all(chunks, axes, split_axis=0, concat_axis=0, tiled=True)
    reduced = jnp.sum(scattered.astype(jnp.float32), axis=0).astype(values.dtype)
    tiled = jnp.broadcast_to(reduced[None], (count,) + reduced.shape)
    gathered = lax.all_to_all(tiled, axes, split_axis=0, concat_axis=0, tiled=True)
    return gathered.reshape(values.shape)


def shards(state_grid, cotangent, legendre, wave_ids, weights):
    lat_count = lax.axis_size("lat")
    lon_count = lax.axis_size("lon")
    samples, rows_dev, lon_cells, channels = state_grid.shape
    slot_count, lat_cells, degree_count = legendre.shape
    slot_reals = 2 * slot_count
    first_slot = (lax.axis_index("lat") * lon_count + lax.axis_index("lon")) * slot_count
    held_waves = lax.dynamic_slice_in_dim(wave_ids, first_slot, slot_count)
    degree_ids = jnp.arange(degree_count, dtype=jnp.int32)
    masked = jnp.where(
        degree_ids[None, None, :] >= held_waves[:, None, None],
        legendre,
        jnp.zeros((), legendre.dtype),
    )
    forward_table, inverse_table = build_tables(wave_ids)
    part_count = 2
    part_slots = slot_count // part_count

    def part_rows(table, part):
        blocks = table.reshape(-1, part_count, 2 * part_slots, table.shape[1])
        return blocks[:, part].reshape(-1, table.shape[1])

    def analyze(source, twiddle, weights_part):
        spectra = jnp.einsum(
            "srnc,kn->srkc", source, twiddle, preferred_element_type=jnp.float32
        ).astype(jnp.bfloat16)
        gathered = lax.all_to_all(spectra, ("lat", "lon"), split_axis=2, concat_axis=1, tiled=True)
        blocks = gathered.reshape(samples, lat_cells, part_slots, 2 * channels)
        spectral = jnp.einsum(
            "samc,mal->slmc", blocks, weights_part, preferred_element_type=jnp.float32
        )
        spectral = spectral.astype(jnp.bfloat16).reshape(
            samples, degree_count, 2 * part_slots, channels
        )
        return lax.all_to_all(spectral, "lat", split_axis=1, concat_axis=2, tiled=True)

    def synthesize(spectral, twiddle, weights_part):
        joined = lax.all_to_all(spectral, "lat", split_axis=2, concat_axis=1, tiled=True)
        blocks = joined.reshape(samples, degree_count, part_slots, 2 * channels)
        spectra = jnp.einsum(
            "slmc,mal->samc", blocks, weights_part, preferred_element_type=jnp.float32
        ).astype(jnp.bfloat16)
        spectra = spectra.reshape(samples, lat_cells, 2 * part_slots, channels)
        pencil = lax.all_to_all(spectra, ("lat", "lon"), split_axis=1, concat_axis=2, tiled=True)
        return jnp.einsum("srkc,kn->srnc", pencil, twiddle, preferred_element_type=jnp.float32)

    real_bd, imag_bd = block_diagonal(weights)
    parts = range(part_count)
    fwd_tables = [part_rows(forward_table, part) for part in parts]
    inv_tables = [part_rows(inverse_table, part) for part in parts]
    masks = [masked[part * part_slots : (part + 1) * part_slots] for part in parts]

    def rolled(values, shift):
        return jnp.roll(values, shift, axis=1)

    coef_parts = []
    branch = None
    for part in parts:
        coef_rows = analyze(state_grid, fwd_tables[part], masks[part])[0]
        row_ids = lax.broadcasted_iota(jnp.int32, coef_rows.shape, 1)
        even_rows = row_ids % 2 == 0
        real_prod = jnp.einsum(
            "lrc,lcd->lrd", coef_rows, real_bd, preferred_element_type=jnp.float32
        )
        imag_prod = jnp.einsum(
            "lrc,lcd->lrd", coef_rows, imag_bd, preferred_element_type=jnp.float32
        )
        mixed_rows = jnp.where(
            even_rows, real_prod - rolled(imag_prod, -1), real_prod + rolled(imag_prod, 1)
        ).astype(jnp.bfloat16)
        partial = synthesize(mixed_rows[None], inv_tables[part], masks[part])
        branch = partial if branch is None else branch + partial
        coef_parts.append(coef_rows)
    pulled = (cotangent.astype(jnp.float32) * gelu_slope(branch)).astype(jnp.bfloat16)
    grad_full = None
    returned = None
    for part in parts:
        coef_rows = coef_parts[part]
        back_rows = analyze(pulled, inv_tables[part], masks[part])[0]
        row_ids = lax.broadcasted_iota(jnp.int32, back_rows.shape, 1)
        even_rows = row_ids % 2 == 0
        swapped = jnp.where(even_rows, rolled(back_rows, -1), -rolled(back_rows, 1))
        grad_part = jnp.einsum(
            "lrc,lrd->lcd",
            coef_rows,
            jnp.concatenate([back_rows, swapped], axis=2),
            preferred_element_type=jnp.float32,
        )
        grad_full = grad_part if grad_full is None else grad_full + grad_part
        real_back = jnp.einsum(
            "lrd,lcd->lrc", back_rows, real_bd, preferred_element_type=jnp.float32
        )
        imag_back = jnp.einsum(
            "lrd,lcd->lrc", back_rows, imag_bd, preferred_element_type=jnp.float32
        )
        demixed_rows = jnp.where(
            even_rows, real_back + rolled(imag_back, -1), real_back - rolled(imag_back, 1)
        ).astype(jnp.bfloat16)
        partial = synthesize(demixed_rows[None], fwd_tables[part], masks[part])
        returned = partial if returned is None else returned + partial
    width = GROUPS * GROUP_WIDTH
    local_grad = jnp.stack(
        [
            jnp.stack(
                [
                    grad_full[
                        :,
                        g * GROUP_WIDTH : (g + 1) * GROUP_WIDTH,
                        t * width + g * GROUP_WIDTH : t * width + (g + 1) * GROUP_WIDTH,
                    ]
                    for g in range(GROUPS)
                ],
                axis=1,
            )
            for t in range(2)
        ],
        axis=1,
    ).reshape(weights.shape)
    weight_grad = reduce_over(local_grad.astype(jnp.bfloat16), ("lon", "dp")).astype(jnp.float32)
    input_grad = (cotangent.astype(jnp.float32) + returned).astype(jnp.bfloat16)
    return (input_grad, weight_grad)


def solution(mesh):
    return jax.shard_map(
        shards,
        mesh=mesh,
        in_specs=(
            P("dp", ("lat", "lon"), None, None),
            P("dp", ("lat", "lon"), None, None),
            P(("lat", "lon"), None, None),
            P(),
            P("lat", None, None, None),
        ),
        out_specs=(P("dp", ("lat", "lon"), None, None), P("lat", None, None, None)),
        check_vma=False,
    )
```

```python
import math

import jax
import jax.numpy as jnp
from jax import lax
from jax.sharding import PartitionSpec as P

NLON = 768
GROUPS = 4
GROUP_WIDTH = 32


def build_tables(wave_ids):
    columns = jnp.arange(NLON, dtype=jnp.int32)
    phase_int = wave_ids[:, None] * columns[None, :] % NLON
    angles = phase_int.astype(jnp.float32) * jnp.float32(2.0 * math.pi / NLON)
    factor = jnp.float32(1.0 / math.sqrt(NLON))
    paired = jnp.stack([jnp.cos(angles) * factor, -jnp.sin(angles) * factor], axis=1)
    forward_table = paired.reshape(2 * wave_ids.shape[0], NLON)
    doubling = jnp.where(wave_ids == 0, 1.0, 2.0).astype(jnp.float32)
    inverse_table = forward_table * jnp.repeat(doubling, 2)[:, None]
    return (forward_table.astype(jnp.bfloat16), inverse_table.astype(jnp.bfloat16))


def block_diagonal(weights):
    degree_count = weights.shape[0]
    width = GROUPS * GROUP_WIDTH
    parts = weights.reshape(degree_count, 2, width, GROUP_WIDTH)
    spread = jnp.tile(parts, (1, 1, 1, GROUPS))
    rows = lax.broadcasted_iota(jnp.int32, (width, width), 0) // GROUP_WIDTH
    cols = lax.broadcasted_iota(jnp.int32, (width, width), 1) // GROUP_WIDTH
    blocks = jnp.where(rows == cols, spread, jnp.zeros((), weights.dtype))
    return blocks[:, 0], blocks[:, 1]


def build_kernel(weights):
    degree_count = weights.shape[0]
    real_part = weights[:, 0].reshape(degree_count, GROUPS, GROUP_WIDTH, GROUP_WIDTH)
    imag_part = weights[:, 1].reshape(degree_count, GROUPS, GROUP_WIDTH, GROUP_WIDTH)
    upper_rows = jnp.stack([real_part, imag_part], axis=3)
    lower_rows = jnp.stack([-imag_part, real_part], axis=3)
    return jnp.stack([upper_rows, lower_rows], axis=2)


def gelu_slope(branch):
    normal_cdf = 0.5 * (1.0 + lax.erf(branch * (1.0 / math.sqrt(2.0))))
    density = jnp.exp(-0.5 * branch * branch) * (1.0 / math.sqrt(2.0 * math.pi))
    return normal_cdf + branch * density


def gather_sum(values, sum_axis, gather_axes):
    parts = lax.axis_size(sum_axis)
    count = 1
    for name in gather_axes:
        count *= lax.axis_size(name)
    rows = values.reshape(-1, values.shape[-1])
    chunks = rows.reshape(parts, rows.shape[0] // parts, rows.shape[1])
    scattered = lax.all_to_all(chunks, sum_axis, split_axis=0, concat_axis=0, tiled=True)
    reduced = jnp.sum(scattered.astype(jnp.float32), axis=0).astype(values.dtype)
    tiled = jnp.broadcast_to(reduced[None], (count,) + reduced.shape)
    gathered = lax.all_to_all(tiled, gather_axes, split_axis=0, concat_axis=0, tiled=True)
    return gathered.reshape(-1, values.shape[-1])


def reduce_over(values, axes):
    count = 1
    for name in axes:
        count *= lax.axis_size(name)
    rows = values.reshape(-1, values.shape[-1])
    chunks = rows.reshape(count, rows.shape[0] // count, rows.shape[1])
    scattered = lax.all_to_all(chunks, axes, split_axis=0, concat_axis=0, tiled=True)
    reduced = jnp.sum(scattered.astype(jnp.float32), axis=0).astype(values.dtype)
    tiled = jnp.broadcast_to(reduced[None], (count,) + reduced.shape)
    gathered = lax.all_to_all(tiled, axes, split_axis=0, concat_axis=0, tiled=True)
    return gathered.reshape(values.shape)


def shards(state_grid, cotangent, legendre, wave_ids, weights):
    lat_count = lax.axis_size("lat")
    lon_count = lax.axis_size("lon")
    samples, rows_dev, lon_cells, channels = state_grid.shape
    slot_count, lat_cells, degree_count = legendre.shape
    slot_reals = 2 * slot_count
    first_slot = (lax.axis_index("lat") * lon_count + lax.axis_index("lon")) * slot_count
    held_waves = lax.dynamic_slice_in_dim(wave_ids, first_slot, slot_count)
    degree_ids = jnp.arange(degree_count, dtype=jnp.int32)
    masked = jnp.where(
        degree_ids[None, None, :] >= held_waves[:, None, None],
        legendre,
        jnp.zeros((), legendre.dtype),
    )
    forward_table, inverse_table = build_tables(wave_ids)

    def analyze(source, twiddle):
        spectra = jnp.einsum(
            "srnc,kn->srkc", source, twiddle, preferred_element_type=jnp.float32
        ).astype(jnp.bfloat16)
        gathered = lax.all_to_all(spectra, ("lat", "lon"), split_axis=2, concat_axis=1, tiled=True)
        blocks = gathered.reshape(samples, lat_cells, slot_count, 2 * channels)
        spectral = jnp.einsum("samc,mal->slmc", blocks, masked, preferred_element_type=jnp.float32)
        spectral = spectral.astype(jnp.bfloat16).reshape(
            samples, degree_count, slot_reals, channels
        )
        return lax.all_to_all(spectral, ("lat", "lon"), split_axis=1, concat_axis=2, tiled=True)

    def synthesize(spectral, twiddle):
        joined = lax.all_to_all(spectral, ("lat", "lon"), split_axis=2, concat_axis=1, tiled=True)
        blocks = joined.reshape(samples, degree_count, slot_count, 2 * channels)
        spectra = jnp.einsum(
            "slmc,mal->samc", blocks, masked, preferred_element_type=jnp.float32
        ).astype(jnp.bfloat16)
        spectra = spectra.reshape(samples, lat_cells, slot_reals, channels)
        pencil = lax.all_to_all(spectra, ("lat", "lon"), split_axis=1, concat_axis=2, tiled=True)
        return jnp.einsum("srkc,kn->srnc", pencil, twiddle, preferred_element_type=jnp.float32)

    coef_fwd = analyze(state_grid, forward_table)
    coef_rows = coef_fwd[0]
    held_count = weights.shape[0] // lon_count
    held_weights = lax.dynamic_slice_in_dim(weights, lax.axis_index("lon") * held_count, held_count)
    real_bd, imag_bd = block_diagonal(held_weights)
    row_ids = lax.broadcasted_iota(jnp.int32, coef_rows.shape, 1)
    even_rows = row_ids % 2 == 0

    def rolled(values, shift):
        return jnp.roll(values, shift, axis=1)

    real_prod = jnp.einsum("lrc,lcd->lrd", coef_rows, real_bd, preferred_element_type=jnp.float32)
    imag_prod = jnp.einsum("lrc,lcd->lrd", coef_rows, imag_bd, preferred_element_type=jnp.float32)
    mixed_rows = jnp.where(
        even_rows, real_prod - rolled(imag_prod, -1), real_prod + rolled(imag_prod, 1)
    ).astype(jnp.bfloat16)
    branch = synthesize(mixed_rows[None], inverse_table)
    pulled = (cotangent.astype(jnp.float32) * gelu_slope(branch)).astype(jnp.bfloat16)
    back_coef = analyze(pulled, inverse_table)
    back_rows = back_coef[0]
    swapped = jnp.where(even_rows, rolled(back_rows, -1), -rolled(back_rows, 1))
    grad_full = jnp.einsum(
        "lrc,lrd->lcd",
        coef_rows,
        jnp.concatenate([back_rows, swapped], axis=2),
        preferred_element_type=jnp.float32,
    )
    width = GROUPS * GROUP_WIDTH
    local_grad = jnp.stack(
        [
            jnp.stack(
                [
                    grad_full[
                        :,
                        g * GROUP_WIDTH : (g + 1) * GROUP_WIDTH,
                        t * width + g * GROUP_WIDTH : t * width + (g + 1) * GROUP_WIDTH,
                    ]
                    for g in range(GROUPS)
                ],
                axis=1,
            )
            for t in range(2)
        ],
        axis=1,
    ).reshape(held_weights.shape)
    weight_grad = gather_sum(local_grad.astype(jnp.bfloat16), "dp", ("lon", "dp"))
    weight_grad = weight_grad.reshape(weights.shape).astype(jnp.float32)
    real_back = jnp.einsum("lrd,lcd->lrc", back_rows, real_bd, preferred_element_type=jnp.float32)
    imag_back = jnp.einsum("lrd,lcd->lrc", back_rows, imag_bd, preferred_element_type=jnp.float32)
    demixed_rows = jnp.where(
        even_rows, real_back + rolled(imag_back, -1), real_back - rolled(imag_back, 1)
    ).astype(jnp.bfloat16)
    returned = synthesize(demixed_rows[None], forward_table)
    input_grad = (cotangent.astype(jnp.float32) + returned).astype(jnp.bfloat16)
    return (input_grad, weight_grad)


def solution(mesh):
    return jax.shard_map(
        shards,
        mesh=mesh,
        in_specs=(
            P("dp", ("lat", "lon"), None, None),
            P("dp", ("lat", "lon"), None, None),
            P(("lat", "lon"), None, None),
            P(),
            P("lat", None, None, None),
        ),
        out_specs=(P("dp", ("lat", "lon"), None, None), P("lat", None, None, None)),
        check_vma=False,
    )
```

```python
import math

import jax
import jax.numpy as jnp
from jax import lax
from jax.sharding import PartitionSpec as P

NLON = 768
GROUPS = 4
GROUP_WIDTH = 32


def build_tables(wave_ids):
    columns = jnp.arange(NLON, dtype=jnp.int32)
    phase_int = wave_ids[:, None] * columns[None, :] % NLON
    angles = phase_int.astype(jnp.float32) * jnp.float32(2.0 * math.pi / NLON)
    factor = jnp.float32(1.0 / math.sqrt(NLON))
    paired = jnp.stack([jnp.cos(angles) * factor, -jnp.sin(angles) * factor], axis=1)
    forward_table = paired.reshape(2 * wave_ids.shape[0], NLON)
    doubling = jnp.where(wave_ids == 0, 1.0, 2.0).astype(jnp.float32)
    inverse_table = forward_table * jnp.repeat(doubling, 2)[:, None]
    return (forward_table.astype(jnp.bfloat16), inverse_table.astype(jnp.bfloat16))


def block_diagonal(weights):
    degree_count = weights.shape[0]
    width = GROUPS * GROUP_WIDTH
    parts = weights.reshape(degree_count, 2, width, GROUP_WIDTH)
    spread = jnp.tile(parts, (1, 1, 1, GROUPS))
    rows = lax.broadcasted_iota(jnp.int32, (width, width), 0) // GROUP_WIDTH
    cols = lax.broadcasted_iota(jnp.int32, (width, width), 1) // GROUP_WIDTH
    blocks = jnp.where(rows == cols, spread, jnp.zeros((), weights.dtype))
    return blocks[:, 0], blocks[:, 1]


def build_kernel(weights):
    degree_count = weights.shape[0]
    real_part = weights[:, 0].reshape(degree_count, GROUPS, GROUP_WIDTH, GROUP_WIDTH)
    imag_part = weights[:, 1].reshape(degree_count, GROUPS, GROUP_WIDTH, GROUP_WIDTH)
    upper_rows = jnp.stack([real_part, imag_part], axis=3)
    lower_rows = jnp.stack([-imag_part, real_part], axis=3)
    return jnp.stack([upper_rows, lower_rows], axis=2)


def gelu_slope(branch):
    normal_cdf = 0.5 * (1.0 + lax.erf(branch * (1.0 / math.sqrt(2.0))))
    density = jnp.exp(-0.5 * branch * branch) * (1.0 / math.sqrt(2.0 * math.pi))
    return normal_cdf + branch * density


def gather_sum(values, sum_axis, gather_axes):
    parts = lax.axis_size(sum_axis)
    count = 1
    for name in gather_axes:
        count *= lax.axis_size(name)
    rows = values.reshape(-1, values.shape[-1])
    chunks = rows.reshape(parts, rows.shape[0] // parts, rows.shape[1])
    scattered = lax.all_to_all(chunks, sum_axis, split_axis=0, concat_axis=0, tiled=True)
    reduced = jnp.sum(scattered.astype(jnp.float32), axis=0).astype(values.dtype)
    tiled = jnp.broadcast_to(reduced[None], (count,) + reduced.shape)
    gathered = lax.all_to_all(tiled, gather_axes, split_axis=0, concat_axis=0, tiled=True)
    return gathered.reshape(-1, values.shape[-1])


def reduce_over(values, axes):
    count = 1
    for name in axes:
        count *= lax.axis_size(name)
    rows = values.reshape(-1, values.shape[-1])
    chunks = rows.reshape(count, rows.shape[0] // count, rows.shape[1])
    scattered = lax.all_to_all(chunks, axes, split_axis=0, concat_axis=0, tiled=True)
    reduced = jnp.sum(scattered.astype(jnp.float32), axis=0).astype(values.dtype)
    tiled = jnp.broadcast_to(reduced[None], (count,) + reduced.shape)
    gathered = lax.all_to_all(tiled, axes, split_axis=0, concat_axis=0, tiled=True)
    return gathered.reshape(values.shape)


def shards(state_grid, cotangent, legendre, wave_ids, weights):
    lat_count = lax.axis_size("lat")
    lon_count = lax.axis_size("lon")
    samples, rows_dev, lon_cells, channels = state_grid.shape
    slot_count, lat_cells, degree_count = legendre.shape
    slot_reals = 2 * slot_count
    first_slot = (lax.axis_index("lat") * lon_count + lax.axis_index("lon")) * slot_count
    held_waves = lax.dynamic_slice_in_dim(wave_ids, first_slot, slot_count)
    degree_ids = jnp.arange(degree_count, dtype=jnp.int32)
    masked = jnp.where(
        degree_ids[None, None, :] >= held_waves[:, None, None],
        legendre,
        jnp.zeros((), legendre.dtype),
    )
    forward_table, inverse_table = build_tables(wave_ids)

    def analyze(source, twiddle):
        spectra = jnp.einsum(
            "srnc,kn->srkc", source, twiddle, preferred_element_type=jnp.float32
        ).astype(jnp.bfloat16)
        gathered = lax.all_to_all(spectra, ("lat", "lon"), split_axis=2, concat_axis=1, tiled=True)
        blocks = gathered.reshape(samples, lat_cells, slot_count, 2 * channels)
        spectral = jnp.einsum("samc,mal->slmc", blocks, masked, preferred_element_type=jnp.float32)
        spectral = spectral.astype(jnp.bfloat16).reshape(
            samples, degree_count, slot_reals, channels
        )
        return lax.all_to_all(spectral, ("lat", "lon"), split_axis=1, concat_axis=2, tiled=True)

    def synthesize(spectral, twiddle):
        joined = lax.all_to_all(spectral, ("lat", "lon"), split_axis=2, concat_axis=1, tiled=True)
        blocks = joined.reshape(samples, degree_count, slot_count, 2 * channels)
        spectra = jnp.einsum(
            "slmc,mal->samc", blocks, masked, preferred_element_type=jnp.float32
        ).astype(jnp.bfloat16)
        spectra = spectra.reshape(samples, lat_cells, slot_reals, channels)
        pencil = lax.all_to_all(spectra, ("lat", "lon"), split_axis=1, concat_axis=2, tiled=True)
        return jnp.einsum("srkc,kn->srnc", pencil, twiddle, preferred_element_type=jnp.float32)

    coef_fwd = analyze(state_grid, forward_table)
    coef_rows = coef_fwd[0]
    held_count = weights.shape[0] // lon_count
    held_weights = lax.dynamic_slice_in_dim(weights, lax.axis_index("lon") * held_count, held_count)
    real_bd, imag_bd = block_diagonal(held_weights)
    row_ids = lax.broadcasted_iota(jnp.int32, coef_rows.shape, 1)
    even_rows = row_ids % 2 == 0

    def rolled(values, shift):
        return jnp.roll(values, shift, axis=1)

    real_prod = jnp.einsum("lrc,lcd->lrd", coef_rows, real_bd, preferred_element_type=jnp.float32)
    imag_prod = jnp.einsum("lrc,lcd->lrd", coef_rows, imag_bd, preferred_element_type=jnp.float32)
    mixed_rows = jnp.where(
        even_rows, real_prod - rolled(imag_prod, -1), real_prod + rolled(imag_prod, 1)
    ).astype(jnp.bfloat16)
    branch = synthesize(mixed_rows[None], inverse_table)
    pulled = (cotangent.astype(jnp.float32) * gelu_slope(branch)).astype(jnp.bfloat16)
    back_coef = analyze(pulled, inverse_table)
    back_rows = back_coef[0]
    swapped = jnp.where(even_rows, rolled(back_rows, -1), -rolled(back_rows, 1))
    grad_full = jnp.einsum(
        "lrc,lrd->lcd",
        coef_rows,
        jnp.concatenate([back_rows, swapped], axis=2),
        preferred_element_type=jnp.float32,
    )
    width = GROUPS * GROUP_WIDTH
    rows_group = lax.broadcasted_iota(jnp.int32, (width, 2 * width), 0) // GROUP_WIDTH
    cols_group = lax.broadcasted_iota(jnp.int32, (width, 2 * width), 1) % width // GROUP_WIDTH
    grad_terms = jnp.where(
        rows_group == cols_group, grad_full.astype(jnp.bfloat16), jnp.zeros((), jnp.bfloat16)
    )
    pick_in = lax.broadcasted_iota(jnp.int32, (2 * width, 2 * GROUP_WIDTH), 0)
    pick_out = lax.broadcasted_iota(jnp.int32, (2 * width, 2 * GROUP_WIDTH), 1)
    picker = (
        (pick_in // width == pick_out // GROUP_WIDTH)
        & (pick_in % GROUP_WIDTH == pick_out % GROUP_WIDTH)
    ).astype(jnp.bfloat16)
    compact = jnp.einsum("lcd,de->lce", grad_terms, picker, preferred_element_type=jnp.float32)
    local_grad = (
        compact.reshape(held_count, GROUPS, GROUP_WIDTH, 2, GROUP_WIDTH)
        .transpose(0, 3, 1, 2, 4)
        .reshape(held_weights.shape)
    )
    weight_grad = gather_sum(local_grad.astype(jnp.bfloat16), "dp", ("lon", "dp"))
    weight_grad = weight_grad.reshape(weights.shape).astype(jnp.float32)
    real_back = jnp.einsum("lrd,lcd->lrc", back_rows, real_bd, preferred_element_type=jnp.float32)
    imag_back = jnp.einsum("lrd,lcd->lrc", back_rows, imag_bd, preferred_element_type=jnp.float32)
    demixed_rows = jnp.where(
        even_rows, real_back + rolled(imag_back, -1), real_back - rolled(imag_back, 1)
    ).astype(jnp.bfloat16)
    returned = synthesize(demixed_rows[None], forward_table)
    input_grad = (cotangent.astype(jnp.float32) + returned).astype(jnp.bfloat16)
    return (input_grad, weight_grad)


def solution(mesh):
    return jax.shard_map(
        shards,
        mesh=mesh,
        in_specs=(
            P("dp", ("lat", "lon"), None, None),
            P("dp", ("lat", "lon"), None, None),
            P(("lat", "lon"), None, None),
            P(),
            P("lat", None, None, None),
        ),
        out_specs=(P("dp", ("lat", "lon"), None, None), P("lat", None, None, None)),
        check_vma=False,
    )
```

```python
import math

import jax
import jax.numpy as jnp
from jax import lax
from jax.sharding import PartitionSpec as P

NLON = 768
GROUPS = 4
GROUP_WIDTH = 32


def build_tables(wave_ids):
    columns = jnp.arange(NLON, dtype=jnp.int32)
    phase_int = wave_ids[:, None] * columns[None, :] % NLON
    angles = phase_int.astype(jnp.float32) * jnp.float32(2.0 * math.pi / NLON)
    factor = jnp.float32(1.0 / math.sqrt(NLON))
    paired = jnp.stack([jnp.cos(angles) * factor, -jnp.sin(angles) * factor], axis=1)
    forward_table = paired.reshape(2 * wave_ids.shape[0], NLON)
    doubling = jnp.where(wave_ids == 0, 1.0, 2.0).astype(jnp.float32)
    inverse_table = forward_table * jnp.repeat(doubling, 2)[:, None]
    return (forward_table.astype(jnp.bfloat16), inverse_table.astype(jnp.bfloat16))


def block_diagonal(weights):
    degree_count = weights.shape[0]
    width = GROUPS * GROUP_WIDTH
    parts = weights.reshape(degree_count, 2, width, GROUP_WIDTH)
    spread = jnp.tile(parts, (1, 1, 1, GROUPS))
    rows = lax.broadcasted_iota(jnp.int32, (width, width), 0) // GROUP_WIDTH
    cols = lax.broadcasted_iota(jnp.int32, (width, width), 1) // GROUP_WIDTH
    blocks = jnp.where(rows == cols, spread, jnp.zeros((), weights.dtype))
    return blocks[:, 0], blocks[:, 1]


def build_kernel(weights):
    degree_count = weights.shape[0]
    real_part = weights[:, 0].reshape(degree_count, GROUPS, GROUP_WIDTH, GROUP_WIDTH)
    imag_part = weights[:, 1].reshape(degree_count, GROUPS, GROUP_WIDTH, GROUP_WIDTH)
    upper_rows = jnp.stack([real_part, imag_part], axis=3)
    lower_rows = jnp.stack([-imag_part, real_part], axis=3)
    return jnp.stack([upper_rows, lower_rows], axis=2)


def gelu_slope(branch):
    normal_cdf = 0.5 * (1.0 + lax.erf(branch * (1.0 / math.sqrt(2.0))))
    density = jnp.exp(-0.5 * branch * branch) * (1.0 / math.sqrt(2.0 * math.pi))
    return normal_cdf + branch * density


def gather_sum(values, sum_axis, gather_axes):
    parts = lax.axis_size(sum_axis)
    count = 1
    for name in gather_axes:
        count *= lax.axis_size(name)
    rows = values.reshape(-1, values.shape[-1])
    chunks = rows.reshape(parts, rows.shape[0] // parts, rows.shape[1])
    scattered = lax.all_to_all(chunks, sum_axis, split_axis=0, concat_axis=0, tiled=True)
    reduced = jnp.sum(scattered.astype(jnp.float32), axis=0).astype(values.dtype)
    gathered = lax.all_gather(reduced, gather_axes, axis=0, tiled=True)
    return gathered.reshape(-1, values.shape[-1])


def reduce_over(values, axes):
    count = 1
    for name in axes:
        count *= lax.axis_size(name)
    rows = values.reshape(-1, values.shape[-1])
    chunks = rows.reshape(count, rows.shape[0] // count, rows.shape[1])
    scattered = lax.all_to_all(chunks, axes, split_axis=0, concat_axis=0, tiled=True)
    reduced = jnp.sum(scattered.astype(jnp.float32), axis=0).astype(values.dtype)
    tiled = jnp.broadcast_to(reduced[None], (count,) + reduced.shape)
    gathered = lax.all_to_all(tiled, axes, split_axis=0, concat_axis=0, tiled=True)
    return gathered.reshape(values.shape)


def shards(state_grid, cotangent, legendre, wave_ids, weights):
    lat_count = lax.axis_size("lat")
    lon_count = lax.axis_size("lon")
    samples, rows_dev, lon_cells, channels = state_grid.shape
    slot_count, lat_cells, degree_count = legendre.shape
    slot_reals = 2 * slot_count
    first_slot = (lax.axis_index("lat") * lon_count + lax.axis_index("lon")) * slot_count
    held_waves = lax.dynamic_slice_in_dim(wave_ids, first_slot, slot_count)
    degree_ids = jnp.arange(degree_count, dtype=jnp.int32)
    masked = jnp.where(
        degree_ids[None, None, :] >= held_waves[:, None, None],
        legendre,
        jnp.zeros((), legendre.dtype),
    )
    forward_table, inverse_table = build_tables(wave_ids)

    def analyze(source, twiddle):
        spectra = jnp.einsum(
            "srnc,kn->srkc", source, twiddle, preferred_element_type=jnp.float32
        ).astype(jnp.bfloat16)
        gathered = lax.all_to_all(spectra, ("lat", "lon"), split_axis=2, concat_axis=1, tiled=True)
        blocks = gathered.reshape(samples, lat_cells, slot_count, 2 * channels)
        spectral = jnp.einsum("samc,mal->slmc", blocks, masked, preferred_element_type=jnp.float32)
        spectral = spectral.astype(jnp.bfloat16).reshape(
            samples, degree_count, slot_reals, channels
        )
        return lax.all_to_all(spectral, ("lat", "lon"), split_axis=1, concat_axis=2, tiled=True)

    def synthesize(spectral, twiddle):
        joined = lax.all_to_all(spectral, ("lat", "lon"), split_axis=2, concat_axis=1, tiled=True)
        blocks = joined.reshape(samples, degree_count, slot_count, 2 * channels)
        spectra = jnp.einsum(
            "slmc,mal->samc", blocks, masked, preferred_element_type=jnp.float32
        ).astype(jnp.bfloat16)
        spectra = spectra.reshape(samples, lat_cells, slot_reals, channels)
        pencil = lax.all_to_all(spectra, ("lat", "lon"), split_axis=1, concat_axis=2, tiled=True)
        return jnp.einsum("srkc,kn->srnc", pencil, twiddle, preferred_element_type=jnp.float32)

    coef_fwd = analyze(state_grid, forward_table)
    coef_rows = coef_fwd[0]
    held_count = weights.shape[0] // lon_count
    held_weights = lax.dynamic_slice_in_dim(weights, lax.axis_index("lon") * held_count, held_count)
    real_bd, imag_bd = block_diagonal(held_weights)
    row_ids = lax.broadcasted_iota(jnp.int32, coef_rows.shape, 1)
    even_rows = row_ids % 2 == 0

    def rolled(values, shift):
        return jnp.roll(values, shift, axis=1)

    real_prod = jnp.einsum("lrc,lcd->lrd", coef_rows, real_bd, preferred_element_type=jnp.float32)
    imag_prod = jnp.einsum("lrc,lcd->lrd", coef_rows, imag_bd, preferred_element_type=jnp.float32)
    mixed_rows = jnp.where(
        even_rows, real_prod - rolled(imag_prod, -1), real_prod + rolled(imag_prod, 1)
    ).astype(jnp.bfloat16)
    branch = synthesize(mixed_rows[None], inverse_table)
    pulled = (cotangent.astype(jnp.float32) * gelu_slope(branch)).astype(jnp.bfloat16)
    back_coef = analyze(pulled, inverse_table)
    back_rows = back_coef[0]
    swapped = jnp.where(even_rows, rolled(back_rows, -1), -rolled(back_rows, 1))
    grad_full = jnp.einsum(
        "lrc,lrd->lcd",
        coef_rows,
        jnp.concatenate([back_rows, swapped], axis=2),
        preferred_element_type=jnp.float32,
    )
    width = GROUPS * GROUP_WIDTH
    rows_group = lax.broadcasted_iota(jnp.int32, (width, 2 * width), 0) // GROUP_WIDTH
    cols_group = lax.broadcasted_iota(jnp.int32, (width, 2 * width), 1) % width // GROUP_WIDTH
    grad_terms = jnp.where(
        rows_group == cols_group, grad_full.astype(jnp.bfloat16), jnp.zeros((), jnp.bfloat16)
    )
    pick_in = lax.broadcasted_iota(jnp.int32, (2 * width, 2 * GROUP_WIDTH), 0)
    pick_out = lax.broadcasted_iota(jnp.int32, (2 * width, 2 * GROUP_WIDTH), 1)
    picker = (
        (pick_in // width == pick_out // GROUP_WIDTH)
        & (pick_in % GROUP_WIDTH == pick_out % GROUP_WIDTH)
    ).astype(jnp.bfloat16)
    compact = jnp.einsum("lcd,de->lce", grad_terms, picker, preferred_element_type=jnp.float32)
    local_grad = (
        compact.reshape(held_count, GROUPS, GROUP_WIDTH, 2, GROUP_WIDTH)
        .transpose(0, 3, 1, 2, 4)
        .reshape(held_weights.shape)
    )
    weight_grad = gather_sum(local_grad.astype(jnp.bfloat16), "dp", ("lon", "dp"))
    weight_grad = weight_grad.reshape(weights.shape).astype(jnp.float32)
    real_back = jnp.einsum("lrd,lcd->lrc", back_rows, real_bd, preferred_element_type=jnp.float32)
    imag_back = jnp.einsum("lrd,lcd->lrc", back_rows, imag_bd, preferred_element_type=jnp.float32)
    demixed_rows = jnp.where(
        even_rows, real_back + rolled(imag_back, -1), real_back - rolled(imag_back, 1)
    ).astype(jnp.bfloat16)
    returned = synthesize(demixed_rows[None], forward_table)
    input_grad = (cotangent.astype(jnp.float32) + returned).astype(jnp.bfloat16)
    return (input_grad, weight_grad)


def solution(mesh):
    return jax.shard_map(
        shards,
        mesh=mesh,
        in_specs=(
            P("dp", ("lat", "lon"), None, None),
            P("dp", ("lat", "lon"), None, None),
            P(("lat", "lon"), None, None),
            P(),
            P("lat", None, None, None),
        ),
        out_specs=(P("dp", ("lat", "lon"), None, None), P("lat", None, None, None)),
        check_vma=False,
    )
```

```python
import math

import jax
import jax.numpy as jnp
from jax import lax
from jax.sharding import PartitionSpec as P

NLON = 768
GROUPS = 4
GROUP_WIDTH = 32


def build_tables(wave_ids):
    columns = jnp.arange(NLON, dtype=jnp.int32)
    phase_int = wave_ids[:, None] * columns[None, :] % NLON
    angles = phase_int.astype(jnp.float32) * jnp.float32(2.0 * math.pi / NLON)
    factor = jnp.float32(1.0 / math.sqrt(NLON))
    paired = jnp.stack([jnp.cos(angles) * factor, -jnp.sin(angles) * factor], axis=1)
    forward_table = paired.reshape(2 * wave_ids.shape[0], NLON)
    doubling = jnp.where(wave_ids == 0, 1.0, 2.0).astype(jnp.float32)
    inverse_table = forward_table * jnp.repeat(doubling, 2)[:, None]
    return (forward_table.astype(jnp.bfloat16), inverse_table.astype(jnp.bfloat16))


def block_diagonal(weights):
    degree_count = weights.shape[0]
    width = GROUPS * GROUP_WIDTH
    parts = weights.reshape(degree_count, 2, width, GROUP_WIDTH)
    spread = jnp.tile(parts, (1, 1, 1, GROUPS))
    rows = lax.broadcasted_iota(jnp.int32, (width, width), 0) // GROUP_WIDTH
    cols = lax.broadcasted_iota(jnp.int32, (width, width), 1) // GROUP_WIDTH
    blocks = jnp.where(rows == cols, spread, jnp.zeros((), weights.dtype))
    return blocks[:, 0], blocks[:, 1]


def build_kernel(weights):
    degree_count = weights.shape[0]
    real_part = weights[:, 0].reshape(degree_count, GROUPS, GROUP_WIDTH, GROUP_WIDTH)
    imag_part = weights[:, 1].reshape(degree_count, GROUPS, GROUP_WIDTH, GROUP_WIDTH)
    upper_rows = jnp.stack([real_part, imag_part], axis=3)
    lower_rows = jnp.stack([-imag_part, real_part], axis=3)
    return jnp.stack([upper_rows, lower_rows], axis=2)


def gelu_slope(branch):
    normal_cdf = 0.5 * (1.0 + lax.erf(branch * (1.0 / math.sqrt(2.0))))
    density = jnp.exp(-0.5 * branch * branch) * (1.0 / math.sqrt(2.0 * math.pi))
    return normal_cdf + branch * density


def gather_sum(values, sum_axis, gather_axes):
    parts = lax.axis_size(sum_axis)
    count = 1
    for name in gather_axes:
        count *= lax.axis_size(name)
    rows = values.reshape(-1, values.shape[-1])
    chunks = rows.reshape(parts, rows.shape[0] // parts, rows.shape[1])
    scattered = lax.all_to_all(chunks, sum_axis, split_axis=0, concat_axis=0, tiled=True)
    reduced = jnp.sum(scattered.astype(jnp.float32), axis=0).astype(values.dtype)
    tiled = jnp.broadcast_to(reduced[None], (count,) + reduced.shape)
    gathered = lax.all_to_all(tiled, gather_axes, split_axis=0, concat_axis=0, tiled=True)
    return gathered.reshape(-1, values.shape[-1])


def reduce_over(values, axes):
    count = 1
    for name in axes:
        count *= lax.axis_size(name)
    rows = values.reshape(-1, values.shape[-1])
    chunks = rows.reshape(count, rows.shape[0] // count, rows.shape[1])
    scattered = lax.all_to_all(chunks, axes, split_axis=0, concat_axis=0, tiled=True)
    reduced = jnp.sum(scattered.astype(jnp.float32), axis=0).astype(values.dtype)
    tiled = jnp.broadcast_to(reduced[None], (count,) + reduced.shape)
    gathered = lax.all_to_all(tiled, axes, split_axis=0, concat_axis=0, tiled=True)
    return gathered.reshape(values.shape)


def shards(state_grid, cotangent, legendre, wave_ids, weights):
    lat_count = lax.axis_size("lat")
    lon_count = lax.axis_size("lon")
    samples, rows_dev, lon_cells, channels = state_grid.shape
    slot_count, lat_cells, degree_count = legendre.shape
    slot_reals = 2 * slot_count
    first_slot = (lax.axis_index("lat") * lon_count + lax.axis_index("lon")) * slot_count
    held_waves = lax.dynamic_slice_in_dim(wave_ids, first_slot, slot_count)
    degree_ids = jnp.arange(degree_count, dtype=jnp.int32)
    masked = jnp.where(
        degree_ids[None, None, :] >= held_waves[:, None, None],
        legendre,
        jnp.zeros((), legendre.dtype),
    )
    forward_table, inverse_table = build_tables(wave_ids)

    def analyze(source, twiddle):
        spectra = jnp.einsum(
            "srnc,kn->srkc", source, twiddle, preferred_element_type=jnp.float32
        ).astype(jnp.bfloat16)
        gathered = lax.all_to_all(spectra, ("lat", "lon"), split_axis=2, concat_axis=1, tiled=True)
        blocks = gathered.reshape(samples, lat_cells, slot_count, 2 * channels)
        spectral = jnp.einsum("samc,mal->slmc", blocks, masked, preferred_element_type=jnp.float32)
        spectral = spectral.astype(jnp.bfloat16).reshape(
            samples, degree_count, slot_reals, channels
        )
        peers = lat_count * lon_count
        spectral = spectral.reshape(peers, degree_count // peers, slot_reals, channels)
        return lax.all_to_all(spectral, ("lat", "lon"), split_axis=0, concat_axis=0, tiled=True)

    def synthesize(spectral, twiddle):
        joined = lax.all_to_all(spectral, ("lat", "lon"), split_axis=0, concat_axis=0, tiled=True)
        blocks = joined.reshape(samples, degree_count, slot_count, 2 * channels)
        spectra = jnp.einsum(
            "slmc,mal->samc", blocks, masked, preferred_element_type=jnp.float32
        ).astype(jnp.bfloat16)
        spectra = spectra.reshape(samples, lat_cells, slot_reals, channels)
        pencil = lax.all_to_all(spectra, ("lat", "lon"), split_axis=1, concat_axis=2, tiled=True)
        return jnp.einsum("srkc,kn->srnc", pencil, twiddle, preferred_element_type=jnp.float32)

    coef_rows = analyze(state_grid, forward_table)
    held_count = weights.shape[0] // lon_count
    held_weights = lax.dynamic_slice_in_dim(weights, lax.axis_index("lon") * held_count, held_count)
    real_bd, imag_bd = block_diagonal(held_weights)
    row_ids = lax.broadcasted_iota(jnp.int32, coef_rows.shape, 2)
    even_rows = row_ids % 2 == 0

    def rolled(values, shift):
        return jnp.roll(values, shift, axis=2)

    real_prod = jnp.einsum("slrc,lcd->slrd", coef_rows, real_bd, preferred_element_type=jnp.float32)
    imag_prod = jnp.einsum("slrc,lcd->slrd", coef_rows, imag_bd, preferred_element_type=jnp.float32)
    mixed_rows = jnp.where(
        even_rows, real_prod - rolled(imag_prod, -1), real_prod + rolled(imag_prod, 1)
    ).astype(jnp.bfloat16)
    branch = synthesize(mixed_rows, inverse_table)
    pulled = (cotangent.astype(jnp.float32) * gelu_slope(branch)).astype(jnp.bfloat16)
    back_rows = analyze(pulled, inverse_table)
    swapped = jnp.where(even_rows, rolled(back_rows, -1), -rolled(back_rows, 1))
    grad_full = jnp.einsum(
        "slrc,slrd->lcd",
        coef_rows,
        jnp.concatenate([back_rows, swapped], axis=3),
        preferred_element_type=jnp.float32,
    )
    width = GROUPS * GROUP_WIDTH
    rows_group = lax.broadcasted_iota(jnp.int32, (width, 2 * width), 0) // GROUP_WIDTH
    cols_group = lax.broadcasted_iota(jnp.int32, (width, 2 * width), 1) % width // GROUP_WIDTH
    grad_terms = jnp.where(
        rows_group == cols_group, grad_full.astype(jnp.bfloat16), jnp.zeros((), jnp.bfloat16)
    )
    pick_in = lax.broadcasted_iota(jnp.int32, (2 * width, 2 * GROUP_WIDTH), 0)
    pick_out = lax.broadcasted_iota(jnp.int32, (2 * width, 2 * GROUP_WIDTH), 1)
    picker = (
        (pick_in // width == pick_out // GROUP_WIDTH)
        & (pick_in % GROUP_WIDTH == pick_out % GROUP_WIDTH)
    ).astype(jnp.bfloat16)
    compact = jnp.einsum("lcd,de->lce", grad_terms, picker, preferred_element_type=jnp.float32)
    local_grad = (
        compact.reshape(held_count, GROUPS, GROUP_WIDTH, 2, GROUP_WIDTH)
        .transpose(0, 3, 1, 2, 4)
        .reshape(held_weights.shape)
    )
    weight_grad = gather_sum(local_grad.astype(jnp.bfloat16), "dp", ("lon", "dp"))
    weight_grad = weight_grad.reshape(weights.shape).astype(jnp.float32)
    real_back = jnp.einsum("slrd,lcd->slrc", back_rows, real_bd, preferred_element_type=jnp.float32)
    imag_back = jnp.einsum("slrd,lcd->slrc", back_rows, imag_bd, preferred_element_type=jnp.float32)
    demixed_rows = jnp.where(
        even_rows, real_back + rolled(imag_back, -1), real_back - rolled(imag_back, 1)
    ).astype(jnp.bfloat16)
    returned = synthesize(demixed_rows, forward_table)
    input_grad = (cotangent.astype(jnp.float32) + returned).astype(jnp.bfloat16)
    return (input_grad, weight_grad)


def solution(mesh):
    return jax.shard_map(
        shards,
        mesh=mesh,
        in_specs=(
            P("dp", ("lat", "lon"), None, None),
            P("dp", ("lat", "lon"), None, None),
            P(("lat", "lon"), None, None),
            P(),
            P("lat", None, None, None),
        ),
        out_specs=(P("dp", ("lat", "lon"), None, None), P("lat", None, None, None)),
        check_vma=False,
    )
```

```python
import math

import jax
import jax.numpy as jnp
from jax import lax
from jax.sharding import PartitionSpec as P

NLON = 768
GROUPS = 4
GROUP_WIDTH = 32


def build_tables(wave_ids):
    columns = jnp.arange(NLON, dtype=jnp.int32)
    phase_int = wave_ids[:, None] * columns[None, :] % NLON
    angles = phase_int.astype(jnp.float32) * jnp.float32(2.0 * math.pi / NLON)
    factor = jnp.float32(1.0 / math.sqrt(NLON))
    paired = jnp.stack([jnp.cos(angles) * factor, -jnp.sin(angles) * factor], axis=1)
    forward_table = paired.reshape(2 * wave_ids.shape[0], NLON)
    doubling = jnp.where(wave_ids == 0, 1.0, 2.0).astype(jnp.float32)
    inverse_table = forward_table * jnp.repeat(doubling, 2)[:, None]
    return (forward_table.astype(jnp.bfloat16), inverse_table.astype(jnp.bfloat16))


def block_diagonal(weights):
    degree_count = weights.shape[0]
    width = GROUPS * GROUP_WIDTH
    parts = weights.reshape(degree_count, 2, width, GROUP_WIDTH)
    spread = jnp.tile(parts, (1, 1, 1, GROUPS))
    rows = lax.broadcasted_iota(jnp.int32, (width, width), 0) // GROUP_WIDTH
    cols = lax.broadcasted_iota(jnp.int32, (width, width), 1) // GROUP_WIDTH
    blocks = jnp.where(rows == cols, spread, jnp.zeros((), weights.dtype))
    return blocks[:, 0], blocks[:, 1]


def build_kernel(weights):
    degree_count = weights.shape[0]
    real_part = weights[:, 0].reshape(degree_count, GROUPS, GROUP_WIDTH, GROUP_WIDTH)
    imag_part = weights[:, 1].reshape(degree_count, GROUPS, GROUP_WIDTH, GROUP_WIDTH)
    upper_rows = jnp.stack([real_part, imag_part], axis=3)
    lower_rows = jnp.stack([-imag_part, real_part], axis=3)
    return jnp.stack([upper_rows, lower_rows], axis=2)


def gelu_slope(branch):
    normal_cdf = 0.5 * (1.0 + lax.erf(branch * (1.0 / math.sqrt(2.0))))
    density = jnp.exp(-0.5 * branch * branch) * (1.0 / math.sqrt(2.0 * math.pi))
    return normal_cdf + branch * density


def gather_sum(values, sum_axis, gather_axes):
    parts = lax.axis_size(sum_axis)
    count = 1
    for name in gather_axes:
        count *= lax.axis_size(name)
    rows = values.reshape(-1, values.shape[-1])
    chunks = rows.reshape(parts, rows.shape[0] // parts, rows.shape[1])
    scattered = lax.all_to_all(chunks, sum_axis, split_axis=0, concat_axis=0, tiled=True)
    reduced = jnp.sum(scattered.astype(jnp.float32), axis=0).astype(values.dtype)
    tiled = jnp.broadcast_to(reduced[None], (count,) + reduced.shape)
    gathered = lax.all_to_all(tiled, gather_axes, split_axis=0, concat_axis=0, tiled=True)
    return gathered.reshape(-1, values.shape[-1])


def reduce_over(values, axes):
    count = 1
    for name in axes:
        count *= lax.axis_size(name)
    rows = values.reshape(-1, values.shape[-1])
    chunks = rows.reshape(count, rows.shape[0] // count, rows.shape[1])
    scattered = lax.all_to_all(chunks, axes, split_axis=0, concat_axis=0, tiled=True)
    reduced = jnp.sum(scattered.astype(jnp.float32), axis=0).astype(values.dtype)
    tiled = jnp.broadcast_to(reduced[None], (count,) + reduced.shape)
    gathered = lax.all_to_all(tiled, axes, split_axis=0, concat_axis=0, tiled=True)
    return gathered.reshape(values.shape)


def shards(state_grid, cotangent, legendre, wave_ids, weights):
    lat_count = lax.axis_size("lat")
    lon_count = lax.axis_size("lon")
    samples, rows_dev, lon_cells, channels = state_grid.shape
    slot_count, lat_cells, degree_count = legendre.shape
    slot_reals = 2 * slot_count
    first_slot = (lax.axis_index("lat") * lon_count + lax.axis_index("lon")) * slot_count
    held_waves = lax.dynamic_slice_in_dim(wave_ids, first_slot, slot_count)
    degree_ids = jnp.arange(degree_count, dtype=jnp.int32)
    masked = jnp.where(
        degree_ids[None, None, :] >= held_waves[:, None, None],
        legendre,
        jnp.zeros((), legendre.dtype),
    )
    forward_table, inverse_table = build_tables(wave_ids)

    def analyze(source, twiddle):
        peers = lat_count * lon_count
        spectra = jnp.einsum(
            "kn,rnc->krc", twiddle, source[0], preferred_element_type=jnp.float32
        ).astype(jnp.bfloat16)
        spectra = spectra.reshape(peers, slot_reals, rows_dev, channels)
        gathered = lax.all_to_all(spectra, ("lat", "lon"), split_axis=0, concat_axis=0, tiled=True)
        blocks = gathered.reshape(peers, slot_count, 2, rows_dev, channels)
        by_source = masked.reshape(slot_count, peers, rows_dev, degree_count)
        spectral = jnp.einsum(
            "smprc,msrl->lmpc", blocks, by_source, preferred_element_type=jnp.float32
        )
        spectral = spectral.astype(jnp.bfloat16).reshape(
            peers, degree_count // peers, slot_reals, channels
        )
        return lax.all_to_all(spectral, ("lat", "lon"), split_axis=0, concat_axis=0, tiled=True)

    def synthesize(spectral, twiddle):
        joined = lax.all_to_all(spectral, ("lat", "lon"), split_axis=0, concat_axis=0, tiled=True)
        blocks = joined.reshape(samples, degree_count, slot_count, 2 * channels)
        spectra = jnp.einsum(
            "slmc,mal->samc", blocks, masked, preferred_element_type=jnp.float32
        ).astype(jnp.bfloat16)
        spectra = spectra.reshape(samples, lat_cells, slot_reals, channels)
        pencil = lax.all_to_all(spectra, ("lat", "lon"), split_axis=1, concat_axis=2, tiled=True)
        return jnp.einsum("srkc,kn->srnc", pencil, twiddle, preferred_element_type=jnp.float32)

    coef_rows = analyze(state_grid, forward_table)
    held_count = weights.shape[0] // lon_count
    held_weights = lax.dynamic_slice_in_dim(weights, lax.axis_index("lon") * held_count, held_count)
    real_bd, imag_bd = block_diagonal(held_weights)
    row_ids = lax.broadcasted_iota(jnp.int32, coef_rows.shape, 2)
    even_rows = row_ids % 2 == 0

    def rolled(values, shift):
        return jnp.roll(values, shift, axis=2)

    real_prod = jnp.einsum("slrc,lcd->slrd", coef_rows, real_bd, preferred_element_type=jnp.float32)
    imag_prod = jnp.einsum("slrc,lcd->slrd", coef_rows, imag_bd, preferred_element_type=jnp.float32)
    mixed_rows = jnp.where(
        even_rows, real_prod - rolled(imag_prod, -1), real_prod + rolled(imag_prod, 1)
    ).astype(jnp.bfloat16)
    branch = synthesize(mixed_rows, inverse_table)
    pulled = (cotangent.astype(jnp.float32) * gelu_slope(branch)).astype(jnp.bfloat16)
    back_rows = analyze(pulled, inverse_table)
    swapped = jnp.where(even_rows, rolled(back_rows, -1), -rolled(back_rows, 1))
    grad_full = jnp.einsum(
        "slrc,slrd->lcd",
        coef_rows,
        jnp.concatenate([back_rows, swapped], axis=3),
        preferred_element_type=jnp.float32,
    )
    width = GROUPS * GROUP_WIDTH
    rows_group = lax.broadcasted_iota(jnp.int32, (width, 2 * width), 0) // GROUP_WIDTH
    cols_group = lax.broadcasted_iota(jnp.int32, (width, 2 * width), 1) % width // GROUP_WIDTH
    grad_terms = jnp.where(
        rows_group == cols_group, grad_full.astype(jnp.bfloat16), jnp.zeros((), jnp.bfloat16)
    )
    pick_in = lax.broadcasted_iota(jnp.int32, (2 * width, 2 * GROUP_WIDTH), 0)
    pick_out = lax.broadcasted_iota(jnp.int32, (2 * width, 2 * GROUP_WIDTH), 1)
    picker = (
        (pick_in // width == pick_out // GROUP_WIDTH)
        & (pick_in % GROUP_WIDTH == pick_out % GROUP_WIDTH)
    ).astype(jnp.bfloat16)
    compact = jnp.einsum("lcd,de->lce", grad_terms, picker, preferred_element_type=jnp.float32)
    local_grad = (
        compact.reshape(held_count, GROUPS, GROUP_WIDTH, 2, GROUP_WIDTH)
        .transpose(0, 3, 1, 2, 4)
        .reshape(held_weights.shape)
    )
    weight_grad = gather_sum(local_grad.astype(jnp.bfloat16), "dp", ("lon", "dp"))
    weight_grad = weight_grad.reshape(weights.shape).astype(jnp.float32)
    real_back = jnp.einsum("slrd,lcd->slrc", back_rows, real_bd, preferred_element_type=jnp.float32)
    imag_back = jnp.einsum("slrd,lcd->slrc", back_rows, imag_bd, preferred_element_type=jnp.float32)
    demixed_rows = jnp.where(
        even_rows, real_back + rolled(imag_back, -1), real_back - rolled(imag_back, 1)
    ).astype(jnp.bfloat16)
    returned = synthesize(demixed_rows, forward_table)
    input_grad = (cotangent.astype(jnp.float32) + returned).astype(jnp.bfloat16)
    return (input_grad, weight_grad)


def solution(mesh):
    return jax.shard_map(
        shards,
        mesh=mesh,
        in_specs=(
            P("dp", ("lat", "lon"), None, None),
            P("dp", ("lat", "lon"), None, None),
            P(("lat", "lon"), None, None),
            P(),
            P("lat", None, None, None),
        ),
        out_specs=(P("dp", ("lat", "lon"), None, None), P("lat", None, None, None)),
        check_vma=False,
    )
```

```python
import math

import jax
import jax.numpy as jnp
from jax import lax
from jax.sharding import PartitionSpec as P

NLON = 768
GROUPS = 4
GROUP_WIDTH = 32


def build_tables(wave_ids):
    slots = wave_ids.shape[0]
    columns = jnp.arange(NLON, dtype=jnp.int32)
    phase_int = wave_ids[:, None] * columns[None, :] % NLON
    angles = phase_int.astype(jnp.float32) * jnp.float32(2.0 * math.pi / NLON)
    factor = jnp.float32(1.0 / math.sqrt(NLON))
    parts = jnp.concatenate(
        [(jnp.cos(angles) * factor).astype(jnp.bfloat16), (-jnp.sin(angles) * factor).astype(jnp.bfloat16)],
        axis=0,
    )
    table_row = lax.broadcasted_iota(jnp.int32, (2 * slots, 2 * slots), 0)
    part_row = lax.broadcasted_iota(jnp.int32, (2 * slots, 2 * slots), 1)
    interleave = (table_row == 2 * (part_row % slots) + part_row // slots).astype(jnp.bfloat16)
    forward_table = jnp.einsum(
        "kj,jn->kn", interleave, parts, preferred_element_type=jnp.float32
    ).astype(jnp.bfloat16)
    doubling = jnp.where(wave_ids == 0, 1.0, 2.0).astype(jnp.bfloat16)
    inverse_table = forward_table * jnp.repeat(doubling, 2)[:, None]
    return (forward_table, inverse_table)


def block_diagonal(weights):
    degree_count = weights.shape[0]
    width = GROUPS * GROUP_WIDTH
    parts = weights.reshape(degree_count, 2, width, GROUP_WIDTH)
    spread = jnp.tile(parts, (1, 1, 1, GROUPS))
    rows = lax.broadcasted_iota(jnp.int32, (width, width), 0) // GROUP_WIDTH
    cols = lax.broadcasted_iota(jnp.int32, (width, width), 1) // GROUP_WIDTH
    blocks = jnp.where(rows == cols, spread, jnp.zeros((), weights.dtype))
    return blocks[:, 0], blocks[:, 1]


def build_kernel(weights):
    degree_count = weights.shape[0]
    real_part = weights[:, 0].reshape(degree_count, GROUPS, GROUP_WIDTH, GROUP_WIDTH)
    imag_part = weights[:, 1].reshape(degree_count, GROUPS, GROUP_WIDTH, GROUP_WIDTH)
    upper_rows = jnp.stack([real_part, imag_part], axis=3)
    lower_rows = jnp.stack([-imag_part, real_part], axis=3)
    return jnp.stack([upper_rows, lower_rows], axis=2)


def gelu_slope(branch):
    normal_cdf = 0.5 * (1.0 + lax.erf(branch * (1.0 / math.sqrt(2.0))))
    density = jnp.exp(-0.5 * branch * branch) * (1.0 / math.sqrt(2.0 * math.pi))
    return normal_cdf + branch * density


def gather_sum(values, sum_axis, gather_axes):
    parts = lax.axis_size(sum_axis)
    count = 1
    for name in gather_axes:
        count *= lax.axis_size(name)
    rows = values.reshape(-1, values.shape[-1])
    chunks = rows.reshape(parts, rows.shape[0] // parts, rows.shape[1])
    scattered = lax.all_to_all(chunks, sum_axis, split_axis=0, concat_axis=0, tiled=True)
    reduced = jnp.sum(scattered.astype(jnp.float32), axis=0).astype(values.dtype)
    tiled = jnp.broadcast_to(reduced[None], (count,) + reduced.shape)
    gathered = lax.all_to_all(tiled, gather_axes, split_axis=0, concat_axis=0, tiled=True)
    return gathered.reshape(-1, values.shape[-1])


def reduce_over(values, axes):
    count = 1
    for name in axes:
        count *= lax.axis_size(name)
    rows = values.reshape(-1, values.shape[-1])
    chunks = rows.reshape(count, rows.shape[0] // count, rows.shape[1])
    scattered = lax.all_to_all(chunks, axes, split_axis=0, concat_axis=0, tiled=True)
    reduced = jnp.sum(scattered.astype(jnp.float32), axis=0).astype(values.dtype)
    tiled = jnp.broadcast_to(reduced[None], (count,) + reduced.shape)
    gathered = lax.all_to_all(tiled, axes, split_axis=0, concat_axis=0, tiled=True)
    return gathered.reshape(values.shape)


def shards(state_grid, cotangent, legendre, wave_ids, weights):
    lat_count = lax.axis_size("lat")
    lon_count = lax.axis_size("lon")
    samples, rows_dev, lon_cells, channels = state_grid.shape
    slot_count, lat_cells, degree_count = legendre.shape
    slot_reals = 2 * slot_count
    first_slot = (lax.axis_index("lat") * lon_count + lax.axis_index("lon")) * slot_count
    held_waves = lax.dynamic_slice_in_dim(wave_ids, first_slot, slot_count)
    degree_ids = jnp.arange(degree_count, dtype=jnp.int32)
    masked = jnp.where(
        degree_ids[None, None, :] >= held_waves[:, None, None],
        legendre,
        jnp.zeros((), legendre.dtype),
    )
    forward_table, inverse_table = build_tables(wave_ids)

    def analyze(source, twiddle):
        spectra = jnp.einsum(
            "srnc,kn->srkc", source, twiddle, preferred_element_type=jnp.float32
        ).astype(jnp.bfloat16)
        gathered = lax.all_to_all(spectra, ("lat", "lon"), split_axis=2, concat_axis=1, tiled=True)
        blocks = gathered.reshape(samples, lat_cells, slot_count, 2 * channels)
        spectral = jnp.einsum("samc,mal->slmc", blocks, masked, preferred_element_type=jnp.float32)
        spectral = spectral.astype(jnp.bfloat16).reshape(
            samples, degree_count, slot_reals, channels
        )
        peers = lat_count * lon_count
        spectral = spectral.reshape(peers, degree_count // peers, slot_reals, channels)
        return lax.all_to_all(spectral, ("lat", "lon"), split_axis=0, concat_axis=0, tiled=True)

    def synthesize(spectral, twiddle):
        joined = lax.all_to_all(spectral, ("lat", "lon"), split_axis=0, concat_axis=0, tiled=True)
        blocks = joined.reshape(samples, degree_count, slot_count, 2 * channels)
        spectra = jnp.einsum(
            "slmc,mal->samc", blocks, masked, preferred_element_type=jnp.float32
        ).astype(jnp.bfloat16)
        spectra = spectra.reshape(samples, lat_cells, slot_reals, channels)
        pencil = lax.all_to_all(spectra, ("lat", "lon"), split_axis=1, concat_axis=2, tiled=True)
        return jnp.einsum("srkc,kn->srnc", pencil, twiddle, preferred_element_type=jnp.float32)

    coef_rows = analyze(state_grid, forward_table)
    held_count = weights.shape[0] // lon_count
    held_weights = lax.dynamic_slice_in_dim(weights, lax.axis_index("lon") * held_count, held_count)
    real_bd, imag_bd = block_diagonal(held_weights)
    row_ids = lax.broadcasted_iota(jnp.int32, coef_rows.shape, 2)
    even_rows = row_ids % 2 == 0

    def rolled(values, shift):
        return jnp.roll(values, shift, axis=2)

    real_prod = jnp.einsum("slrc,lcd->slrd", coef_rows, real_bd, preferred_element_type=jnp.float32)
    imag_prod = jnp.einsum("slrc,lcd->slrd", coef_rows, imag_bd, preferred_element_type=jnp.float32)
    mixed_rows = jnp.where(
        even_rows, real_prod - rolled(imag_prod, -1), real_prod + rolled(imag_prod, 1)
    ).astype(jnp.bfloat16)
    branch = synthesize(mixed_rows, inverse_table)
    pulled = (cotangent.astype(jnp.float32) * gelu_slope(branch)).astype(jnp.bfloat16)
    back_rows = analyze(pulled, inverse_table)
    swapped = jnp.where(even_rows, rolled(back_rows, -1), -rolled(back_rows, 1))
    grad_full = jnp.einsum(
        "slrc,slrd->lcd",
        coef_rows,
        jnp.concatenate([back_rows, swapped], axis=3),
        preferred_element_type=jnp.float32,
    )
    width = GROUPS * GROUP_WIDTH
    rows_group = lax.broadcasted_iota(jnp.int32, (width, 2 * width), 0) // GROUP_WIDTH
    cols_group = lax.broadcasted_iota(jnp.int32, (width, 2 * width), 1) % width // GROUP_WIDTH
    grad_terms = jnp.where(
        rows_group == cols_group, grad_full.astype(jnp.bfloat16), jnp.zeros((), jnp.bfloat16)
    )
    pick_in = lax.broadcasted_iota(jnp.int32, (2 * width, 2 * GROUP_WIDTH), 0)
    pick_out = lax.broadcasted_iota(jnp.int32, (2 * width, 2 * GROUP_WIDTH), 1)
    picker = (
        (pick_in // width == pick_out // GROUP_WIDTH)
        & (pick_in % GROUP_WIDTH == pick_out % GROUP_WIDTH)
    ).astype(jnp.bfloat16)
    compact = jnp.einsum("lcd,de->lce", grad_terms, picker, preferred_element_type=jnp.float32)
    local_grad = (
        compact.reshape(held_count, GROUPS, GROUP_WIDTH, 2, GROUP_WIDTH)
        .transpose(0, 3, 1, 2, 4)
        .reshape(held_weights.shape)
    )
    weight_grad = gather_sum(local_grad.astype(jnp.bfloat16), "dp", ("lon", "dp"))
    weight_grad = weight_grad.reshape(weights.shape).astype(jnp.float32)
    real_back = jnp.einsum("slrd,lcd->slrc", back_rows, real_bd, preferred_element_type=jnp.float32)
    imag_back = jnp.einsum("slrd,lcd->slrc", back_rows, imag_bd, preferred_element_type=jnp.float32)
    demixed_rows = jnp.where(
        even_rows, real_back + rolled(imag_back, -1), real_back - rolled(imag_back, 1)
    ).astype(jnp.bfloat16)
    returned = synthesize(demixed_rows, forward_table)
    input_grad = (cotangent.astype(jnp.float32) + returned).astype(jnp.bfloat16)
    return (input_grad, weight_grad)


def solution(mesh):
    return jax.shard_map(
        shards,
        mesh=mesh,
        in_specs=(
            P("dp", ("lat", "lon"), None, None),
            P("dp", ("lat", "lon"), None, None),
            P(("lat", "lon"), None, None),
            P(),
            P("lat", None, None, None),
        ),
        out_specs=(P("dp", ("lat", "lon"), None, None), P("lat", None, None, None)),
        check_vma=False,
    )
```

```python
import math

import jax
import jax.numpy as jnp
from jax import lax
from jax.sharding import PartitionSpec as P

NLON = 768
GROUPS = 4
GROUP_WIDTH = 32


def build_tables(wave_ids):
    slots = wave_ids.shape[0]
    columns = jnp.arange(NLON, dtype=jnp.int32)
    phase_int = wave_ids[:, None] * columns[None, :] % NLON
    angles = phase_int.astype(jnp.float32) * jnp.float32(2.0 * math.pi / NLON)
    factor = jnp.float32(1.0 / math.sqrt(NLON))
    parts = jnp.concatenate(
        [(jnp.cos(angles) * factor).astype(jnp.bfloat16), (-jnp.sin(angles) * factor).astype(jnp.bfloat16)],
        axis=0,
    )
    table_row = lax.broadcasted_iota(jnp.int32, (2 * slots, 2 * slots), 0)
    part_row = lax.broadcasted_iota(jnp.int32, (2 * slots, 2 * slots), 1)
    interleave = (table_row == 2 * (part_row % slots) + part_row // slots).astype(jnp.bfloat16)
    forward_table = jnp.einsum(
        "kj,jn->kn", interleave, parts, preferred_element_type=jnp.float32
    ).astype(jnp.bfloat16)
    doubling = jnp.where(wave_ids == 0, 1.0, 2.0).astype(jnp.bfloat16)
    inverse_table = forward_table * jnp.repeat(doubling, 2)[:, None]
    return (forward_table, inverse_table)


def block_diagonal(weights):
    degree_count = weights.shape[0]
    width = GROUPS * GROUP_WIDTH
    parts = weights.reshape(degree_count, 2, width, GROUP_WIDTH)
    spread = jnp.tile(parts, (1, 1, 1, GROUPS))
    rows = lax.broadcasted_iota(jnp.int32, (width, width), 0) // GROUP_WIDTH
    cols = lax.broadcasted_iota(jnp.int32, (width, width), 1) // GROUP_WIDTH
    blocks = jnp.where(rows == cols, spread, jnp.zeros((), weights.dtype))
    return blocks[:, 0], blocks[:, 1]


def build_kernel(weights):
    degree_count = weights.shape[0]
    real_part = weights[:, 0].reshape(degree_count, GROUPS, GROUP_WIDTH, GROUP_WIDTH)
    imag_part = weights[:, 1].reshape(degree_count, GROUPS, GROUP_WIDTH, GROUP_WIDTH)
    upper_rows = jnp.stack([real_part, imag_part], axis=3)
    lower_rows = jnp.stack([-imag_part, real_part], axis=3)
    return jnp.stack([upper_rows, lower_rows], axis=2)


def gelu_slope(branch):
    normal_cdf = 0.5 * (1.0 + lax.erf(branch * (1.0 / math.sqrt(2.0))))
    density = jnp.exp(-0.5 * branch * branch) * (1.0 / math.sqrt(2.0 * math.pi))
    return normal_cdf + branch * density


def gather_sum(values, sum_axis, gather_axes):
    parts = lax.axis_size(sum_axis)
    count = 1
    for name in gather_axes:
        count *= lax.axis_size(name)
    rows = values.reshape(-1, values.shape[-1])
    chunks = rows.reshape(parts, rows.shape[0] // parts, rows.shape[1])
    scattered = lax.all_to_all(chunks, sum_axis, split_axis=0, concat_axis=0, tiled=True)
    reduced = jnp.sum(scattered.astype(jnp.float32), axis=0).astype(values.dtype)
    tiled = jnp.broadcast_to(reduced[None], (count,) + reduced.shape)
    gathered = lax.all_to_all(tiled, gather_axes, split_axis=0, concat_axis=0, tiled=True)
    return gathered.reshape(-1, values.shape[-1])


def reduce_over(values, axes):
    count = 1
    for name in axes:
        count *= lax.axis_size(name)
    rows = values.reshape(-1, values.shape[-1])
    chunks = rows.reshape(count, rows.shape[0] // count, rows.shape[1])
    scattered = lax.all_to_all(chunks, axes, split_axis=0, concat_axis=0, tiled=True)
    reduced = jnp.sum(scattered.astype(jnp.float32), axis=0).astype(values.dtype)
    tiled = jnp.broadcast_to(reduced[None], (count,) + reduced.shape)
    gathered = lax.all_to_all(tiled, axes, split_axis=0, concat_axis=0, tiled=True)
    return gathered.reshape(values.shape)


def shards(state_grid, cotangent, legendre, wave_ids, weights):
    lat_count = lax.axis_size("lat")
    lon_count = lax.axis_size("lon")
    samples, rows_dev, lon_cells, channels = state_grid.shape
    slot_count, lat_cells, degree_count = legendre.shape
    slot_reals = 2 * slot_count
    first_slot = (lax.axis_index("lat") * lon_count + lax.axis_index("lon")) * slot_count
    held_waves = lax.dynamic_slice_in_dim(wave_ids, first_slot, slot_count)
    degree_ids = jnp.arange(degree_count, dtype=jnp.int32)
    masked = jnp.where(
        degree_ids[None, None, :] >= held_waves[:, None, None],
        legendre,
        jnp.zeros((), legendre.dtype),
    )
    forward_table, inverse_table = build_tables(wave_ids)

    def analyze(source, twiddle):
        spectra = jnp.einsum(
            "srnc,kn->srkc", source, twiddle, preferred_element_type=jnp.float32
        ).astype(jnp.bfloat16)
        gathered = lax.all_to_all(spectra, ("lat", "lon"), split_axis=2, concat_axis=1, tiled=True)
        blocks = gathered.reshape(samples, lat_cells, slot_count, 2 * channels)
        spectral = jnp.einsum("samc,mal->slmc", blocks, masked, preferred_element_type=jnp.float32)
        peers = lat_count * lon_count
        spectral = spectral.astype(jnp.bfloat16).reshape(
            peers, degree_count // peers, slot_count, 2 * channels
        )
        return lax.all_to_all(spectral, ("lat", "lon"), split_axis=0, concat_axis=0, tiled=True)

    def synthesize(spectral, twiddle):
        joined = lax.all_to_all(spectral, ("lat", "lon"), split_axis=0, concat_axis=0, tiled=True)
        blocks = joined.reshape(samples, degree_count, slot_count, 2 * channels)
        spectra = jnp.einsum(
            "slmc,mal->samc", blocks, masked, preferred_element_type=jnp.float32
        ).astype(jnp.bfloat16)
        spectra = spectra.reshape(samples, lat_cells, slot_reals, channels)
        pencil = lax.all_to_all(spectra, ("lat", "lon"), split_axis=1, concat_axis=2, tiled=True)
        return jnp.einsum("srkc,kn->srnc", pencil, twiddle, preferred_element_type=jnp.float32)

    coef_rows = analyze(state_grid, forward_table)
    held_count = weights.shape[0] // lon_count
    held_weights = lax.dynamic_slice_in_dim(weights, lax.axis_index("lon") * held_count, held_count)
    real_bd, imag_bd = block_diagonal(held_weights)
    mixing = jnp.concatenate(
        [
            jnp.concatenate([real_bd, imag_bd], axis=2),
            jnp.concatenate([-imag_bd, real_bd], axis=2),
        ],
        axis=1,
    )
    mixed_rows = jnp.einsum(
        "slmc,lcd->slmd", coef_rows, mixing, preferred_element_type=jnp.float32
    ).astype(jnp.bfloat16)
    branch = synthesize(mixed_rows, inverse_table)
    pulled = (cotangent.astype(jnp.float32) * gelu_slope(branch)).astype(jnp.bfloat16)
    back_rows = analyze(pulled, inverse_table)
    pair_products = jnp.einsum(
        "slmc,slmd->lcd", coef_rows, back_rows, preferred_element_type=jnp.float32
    )
    width = GROUPS * GROUP_WIDTH
    same_part = pair_products[:, :width, :width] + pair_products[:, width:, width:]
    cross_part = pair_products[:, :width, width:] - pair_products[:, width:, :width]
    grad_full = jnp.concatenate([same_part, cross_part], axis=2)
    rows_group = lax.broadcasted_iota(jnp.int32, (width, 2 * width), 0) // GROUP_WIDTH
    cols_group = lax.broadcasted_iota(jnp.int32, (width, 2 * width), 1) % width // GROUP_WIDTH
    grad_terms = jnp.where(
        rows_group == cols_group, grad_full.astype(jnp.bfloat16), jnp.zeros((), jnp.bfloat16)
    )
    pick_in = lax.broadcasted_iota(jnp.int32, (2 * width, 2 * GROUP_WIDTH), 0)
    pick_out = lax.broadcasted_iota(jnp.int32, (2 * width, 2 * GROUP_WIDTH), 1)
    picker = (
        (pick_in // width == pick_out // GROUP_WIDTH)
        & (pick_in % GROUP_WIDTH == pick_out % GROUP_WIDTH)
    ).astype(jnp.bfloat16)
    compact = jnp.einsum("lcd,de->lce", grad_terms, picker, preferred_element_type=jnp.float32)
    local_grad = (
        compact.reshape(held_count, GROUPS, GROUP_WIDTH, 2, GROUP_WIDTH)
        .transpose(0, 3, 1, 2, 4)
        .reshape(held_weights.shape)
    )
    weight_grad = gather_sum(local_grad.astype(jnp.bfloat16), "dp", ("lon", "dp"))
    weight_grad = weight_grad.reshape(weights.shape).astype(jnp.float32)
    demixed_rows = jnp.einsum(
        "slmd,lcd->slmc", back_rows, mixing, preferred_element_type=jnp.float32
    ).astype(jnp.bfloat16)
    returned = synthesize(demixed_rows, forward_table)
    input_grad = (cotangent.astype(jnp.float32) + returned).astype(jnp.bfloat16)
    return (input_grad, weight_grad)


def solution(mesh):
    return jax.shard_map(
        shards,
        mesh=mesh,
        in_specs=(
            P("dp", ("lat", "lon"), None, None),
            P("dp", ("lat", "lon"), None, None),
            P(("lat", "lon"), None, None),
            P(),
            P("lat", None, None, None),
        ),
        out_specs=(P("dp", ("lat", "lon"), None, None), P("lat", None, None, None)),
        check_vma=False,
    )
```

```python
import math

import jax
import jax.numpy as jnp
from jax import lax
from jax.sharding import PartitionSpec as P

NLON = 768
GROUPS = 4
GROUP_WIDTH = 32


def build_tables(wave_ids):
    slots = wave_ids.shape[0]
    columns = jnp.arange(NLON, dtype=jnp.int32)
    phase_int = wave_ids[:, None] * columns[None, :] % NLON
    angles = phase_int.astype(jnp.float32) * jnp.float32(2.0 * math.pi / NLON)
    factor = jnp.float32(1.0 / math.sqrt(NLON))
    parts = jnp.concatenate(
        [(jnp.cos(angles) * factor).astype(jnp.bfloat16), (-jnp.sin(angles) * factor).astype(jnp.bfloat16)],
        axis=0,
    )
    table_row = lax.broadcasted_iota(jnp.int32, (2 * slots, 2 * slots), 0)
    part_row = lax.broadcasted_iota(jnp.int32, (2 * slots, 2 * slots), 1)
    interleave = (table_row == 2 * (part_row % slots) + part_row // slots).astype(jnp.bfloat16)
    forward_table = jnp.einsum(
        "kj,jn->kn", interleave, parts, preferred_element_type=jnp.float32
    ).astype(jnp.bfloat16)
    doubling = jnp.where(wave_ids == 0, 1.0, 2.0).astype(jnp.bfloat16)
    inverse_table = forward_table * jnp.repeat(doubling, 2)[:, None]
    return (forward_table, inverse_table)


def block_diagonal(weights):
    degree_count = weights.shape[0]
    width = GROUPS * GROUP_WIDTH
    parts = weights.reshape(degree_count, 2, width, GROUP_WIDTH)
    spread = jnp.tile(parts, (1, 1, 1, GROUPS))
    rows = lax.broadcasted_iota(jnp.int32, (width, width), 0) // GROUP_WIDTH
    cols = lax.broadcasted_iota(jnp.int32, (width, width), 1) // GROUP_WIDTH
    blocks = jnp.where(rows == cols, spread, jnp.zeros((), weights.dtype))
    return blocks[:, 0], blocks[:, 1]


def build_kernel(weights):
    degree_count = weights.shape[0]
    real_part = weights[:, 0].reshape(degree_count, GROUPS, GROUP_WIDTH, GROUP_WIDTH)
    imag_part = weights[:, 1].reshape(degree_count, GROUPS, GROUP_WIDTH, GROUP_WIDTH)
    upper_rows = jnp.stack([real_part, imag_part], axis=3)
    lower_rows = jnp.stack([-imag_part, real_part], axis=3)
    return jnp.stack([upper_rows, lower_rows], axis=2)


def gelu_slope(branch):
    normal_cdf = 0.5 * (1.0 + lax.erf(branch * (1.0 / math.sqrt(2.0))))
    density = jnp.exp(-0.5 * branch * branch) * (1.0 / math.sqrt(2.0 * math.pi))
    return normal_cdf + branch * density


def gather_after_sum(values, sum_axis, gather_axes):
    count = 1
    for name in gather_axes:
        count *= lax.axis_size(name)
    parts = lax.axis_size(sum_axis)
    rows = lax.psum(values, sum_axis).reshape(-1, values.shape[-1])
    own = rows.reshape(parts, rows.shape[0] // parts, rows.shape[1])
    mine = lax.dynamic_index_in_dim(own, lax.axis_index(sum_axis), 0, keepdims=False)
    tiled = jnp.broadcast_to(mine[None], (count,) + mine.shape)
    gathered = lax.all_to_all(tiled, gather_axes, split_axis=0, concat_axis=0, tiled=True)
    return gathered.reshape(-1, values.shape[-1])


def gather_sum(values, sum_axis, gather_axes):
    parts = lax.axis_size(sum_axis)
    count = 1
    for name in gather_axes:
        count *= lax.axis_size(name)
    rows = values.reshape(-1, values.shape[-1])
    chunks = rows.reshape(parts, rows.shape[0] // parts, rows.shape[1])
    scattered = lax.all_to_all(chunks, sum_axis, split_axis=0, concat_axis=0, tiled=True)
    reduced = jnp.sum(scattered.astype(jnp.float32), axis=0).astype(values.dtype)
    tiled = jnp.broadcast_to(reduced[None], (count,) + reduced.shape)
    gathered = lax.all_to_all(tiled, gather_axes, split_axis=0, concat_axis=0, tiled=True)
    return gathered.reshape(-1, values.shape[-1])


def reduce_over(values, axes):
    count = 1
    for name in axes:
        count *= lax.axis_size(name)
    rows = values.reshape(-1, values.shape[-1])
    chunks = rows.reshape(count, rows.shape[0] // count, rows.shape[1])
    scattered = lax.all_to_all(chunks, axes, split_axis=0, concat_axis=0, tiled=True)
    reduced = jnp.sum(scattered.astype(jnp.float32), axis=0).astype(values.dtype)
    tiled = jnp.broadcast_to(reduced[None], (count,) + reduced.shape)
    gathered = lax.all_to_all(tiled, axes, split_axis=0, concat_axis=0, tiled=True)
    return gathered.reshape(values.shape)


def shards(state_grid, cotangent, legendre, wave_ids, weights):
    lat_count = lax.axis_size("lat")
    lon_count = lax.axis_size("lon")
    samples, rows_dev, lon_cells, channels = state_grid.shape
    slot_count, lat_cells, degree_count = legendre.shape
    slot_reals = 2 * slot_count
    first_slot = (lax.axis_index("lat") * lon_count + lax.axis_index("lon")) * slot_count
    held_waves = lax.dynamic_slice_in_dim(wave_ids, first_slot, slot_count)
    degree_ids = jnp.arange(degree_count, dtype=jnp.int32)
    masked = jnp.where(
        degree_ids[None, None, :] >= held_waves[:, None, None],
        legendre,
        jnp.zeros((), legendre.dtype),
    )
    forward_table, inverse_table = build_tables(wave_ids)

    def analyze(source, twiddle):
        spectra = jnp.einsum(
            "srnc,kn->srkc", source, twiddle, preferred_element_type=jnp.float32
        ).astype(jnp.bfloat16)
        gathered = lax.all_to_all(spectra, ("lat", "lon"), split_axis=2, concat_axis=1, tiled=True)
        blocks = gathered.reshape(samples, lat_cells, slot_count, 2 * channels)
        spectral = jnp.einsum("samc,mal->slmc", blocks, masked, preferred_element_type=jnp.float32)
        peers = lat_count * lon_count
        spectral = spectral.astype(jnp.bfloat16).reshape(
            peers, degree_count // peers, slot_count, 2 * channels
        )
        return lax.all_to_all(spectral, ("lat", "lon"), split_axis=0, concat_axis=0, tiled=True)

    def synthesize(spectral, twiddle):
        joined = lax.all_to_all(spectral, ("lat", "lon"), split_axis=0, concat_axis=0, tiled=True)
        blocks = joined.reshape(samples, degree_count, slot_count, 2 * channels)
        spectra = jnp.einsum(
            "slmc,mal->samc", blocks, masked, preferred_element_type=jnp.float32
        ).astype(jnp.bfloat16)
        spectra = spectra.reshape(samples, lat_cells, slot_reals, channels)
        pencil = lax.all_to_all(spectra, ("lat", "lon"), split_axis=1, concat_axis=2, tiled=True)
        return jnp.einsum("srkc,kn->srnc", pencil, twiddle, preferred_element_type=jnp.float32)

    coef_rows = analyze(state_grid, forward_table)
    held_count = weights.shape[0] // lon_count
    held_weights = lax.dynamic_slice_in_dim(weights, lax.axis_index("lon") * held_count, held_count)
    real_bd, imag_bd = block_diagonal(held_weights)
    mixing = jnp.concatenate(
        [
            jnp.concatenate([real_bd, imag_bd], axis=2),
            jnp.concatenate([-imag_bd, real_bd], axis=2),
        ],
        axis=1,
    )
    mixed_rows = jnp.einsum(
        "slmc,lcd->slmd", coef_rows, mixing, preferred_element_type=jnp.float32
    ).astype(jnp.bfloat16)
    branch = synthesize(mixed_rows, inverse_table)
    pulled = (cotangent.astype(jnp.float32) * gelu_slope(branch)).astype(jnp.bfloat16)
    back_rows = analyze(pulled, inverse_table)
    pair_products = jnp.einsum(
        "slmc,slmd->lcd", coef_rows, back_rows, preferred_element_type=jnp.float32
    )
    width = GROUPS * GROUP_WIDTH
    same_part = pair_products[:, :width, :width] + pair_products[:, width:, width:]
    cross_part = pair_products[:, :width, width:] - pair_products[:, width:, :width]
    grad_full = jnp.concatenate([same_part, cross_part], axis=2)
    rows_group = lax.broadcasted_iota(jnp.int32, (width, 2 * width), 0) // GROUP_WIDTH
    cols_group = lax.broadcasted_iota(jnp.int32, (width, 2 * width), 1) % width // GROUP_WIDTH
    grad_terms = jnp.where(
        rows_group == cols_group, grad_full.astype(jnp.bfloat16), jnp.zeros((), jnp.bfloat16)
    )
    pick_in = lax.broadcasted_iota(jnp.int32, (2 * width, 2 * GROUP_WIDTH), 0)
    pick_out = lax.broadcasted_iota(jnp.int32, (2 * width, 2 * GROUP_WIDTH), 1)
    picker = (
        (pick_in // width == pick_out // GROUP_WIDTH)
        & (pick_in % GROUP_WIDTH == pick_out % GROUP_WIDTH)
    ).astype(jnp.bfloat16)
    compact = jnp.einsum("lcd,de->lce", grad_terms, picker, preferred_element_type=jnp.float32)
    local_grad = (
        compact.reshape(held_count, GROUPS, GROUP_WIDTH, 2, GROUP_WIDTH)
        .transpose(0, 3, 1, 2, 4)
        .reshape(held_weights.shape)
    )
    weight_grad = gather_after_sum(local_grad.astype(jnp.bfloat16), "dp", ("lon", "dp"))
    weight_grad = weight_grad.reshape(weights.shape).astype(jnp.float32)
    demixed_rows = jnp.einsum(
        "slmd,lcd->slmc", back_rows, mixing, preferred_element_type=jnp.float32
    ).astype(jnp.bfloat16)
    returned = synthesize(demixed_rows, forward_table)
    input_grad = (cotangent.astype(jnp.float32) + returned).astype(jnp.bfloat16)
    return (input_grad, weight_grad)


def solution(mesh):
    return jax.shard_map(
        shards,
        mesh=mesh,
        in_specs=(
            P("dp", ("lat", "lon"), None, None),
            P("dp", ("lat", "lon"), None, None),
            P(("lat", "lon"), None, None),
            P(),
            P("lat", None, None, None),
        ),
        out_specs=(P("dp", ("lat", "lon"), None, None), P("lat", None, None, None)),
        check_vma=False,
    )
```

```python
import math

import jax
import jax.numpy as jnp
from jax import lax
from jax.sharding import PartitionSpec as P

NLON = 768
GROUPS = 4
GROUP_WIDTH = 32


def build_tables(wave_ids):
    slots = wave_ids.shape[0]
    columns = jnp.arange(NLON, dtype=jnp.int32)
    phase_int = wave_ids[:, None] * columns[None, :] % NLON
    angles = columns.astype(jnp.float32) * jnp.float32(2.0 * math.pi / NLON)
    factor = jnp.float32(1.0 / math.sqrt(NLON))
    lookup = jnp.concatenate(
        [(jnp.cos(angles) * factor).astype(jnp.bfloat16), (-jnp.sin(angles) * factor).astype(jnp.bfloat16)]
    )
    parts = jnp.take(
        lookup, jnp.concatenate([phase_int, phase_int + NLON], axis=0), mode="clip"
    )
    table_row = lax.broadcasted_iota(jnp.int32, (2 * slots, 2 * slots), 0)
    part_row = lax.broadcasted_iota(jnp.int32, (2 * slots, 2 * slots), 1)
    interleave = (table_row == 2 * (part_row % slots) + part_row // slots).astype(jnp.bfloat16)
    forward_table = jnp.einsum(
        "kj,jn->kn", interleave, parts, preferred_element_type=jnp.float32
    ).astype(jnp.bfloat16)
    doubling = jnp.where(wave_ids == 0, 1.0, 2.0).astype(jnp.bfloat16)
    inverse_table = forward_table * jnp.repeat(doubling, 2)[:, None]
    return (forward_table, inverse_table)


def block_diagonal(weights):
    degree_count = weights.shape[0]
    width = GROUPS * GROUP_WIDTH
    parts = weights.reshape(degree_count, 2, width, GROUP_WIDTH)
    spread = jnp.tile(parts, (1, 1, 1, GROUPS))
    rows = lax.broadcasted_iota(jnp.int32, (width, width), 0) // GROUP_WIDTH
    cols = lax.broadcasted_iota(jnp.int32, (width, width), 1) // GROUP_WIDTH
    blocks = jnp.where(rows == cols, spread, jnp.zeros((), weights.dtype))
    return blocks[:, 0], blocks[:, 1]


def build_kernel(weights):
    degree_count = weights.shape[0]
    real_part = weights[:, 0].reshape(degree_count, GROUPS, GROUP_WIDTH, GROUP_WIDTH)
    imag_part = weights[:, 1].reshape(degree_count, GROUPS, GROUP_WIDTH, GROUP_WIDTH)
    upper_rows = jnp.stack([real_part, imag_part], axis=3)
    lower_rows = jnp.stack([-imag_part, real_part], axis=3)
    return jnp.stack([upper_rows, lower_rows], axis=2)


def gelu_slope(branch):
    normal_cdf = 0.5 * (1.0 + lax.erf(branch * (1.0 / math.sqrt(2.0))))
    density = jnp.exp(-0.5 * branch * branch) * (1.0 / math.sqrt(2.0 * math.pi))
    return normal_cdf + branch * density


def gather_sum(values, sum_axis, gather_axes):
    parts = lax.axis_size(sum_axis)
    count = 1
    for name in gather_axes:
        count *= lax.axis_size(name)
    rows = values.reshape(-1, values.shape[-1])
    chunks = rows.reshape(parts, rows.shape[0] // parts, rows.shape[1])
    scattered = lax.all_to_all(chunks, sum_axis, split_axis=0, concat_axis=0, tiled=True)
    reduced = jnp.sum(scattered.astype(jnp.float32), axis=0).astype(values.dtype)
    tiled = jnp.broadcast_to(reduced[None], (count,) + reduced.shape)
    gathered = lax.all_to_all(tiled, gather_axes, split_axis=0, concat_axis=0, tiled=True)
    return gathered.reshape(-1, values.shape[-1])


def reduce_over(values, axes):
    count = 1
    for name in axes:
        count *= lax.axis_size(name)
    rows = values.reshape(-1, values.shape[-1])
    chunks = rows.reshape(count, rows.shape[0] // count, rows.shape[1])
    scattered = lax.all_to_all(chunks, axes, split_axis=0, concat_axis=0, tiled=True)
    reduced = jnp.sum(scattered.astype(jnp.float32), axis=0).astype(values.dtype)
    tiled = jnp.broadcast_to(reduced[None], (count,) + reduced.shape)
    gathered = lax.all_to_all(tiled, axes, split_axis=0, concat_axis=0, tiled=True)
    return gathered.reshape(values.shape)


def shards(state_grid, cotangent, legendre, wave_ids, weights):
    lat_count = lax.axis_size("lat")
    lon_count = lax.axis_size("lon")
    samples, rows_dev, lon_cells, channels = state_grid.shape
    slot_count, lat_cells, degree_count = legendre.shape
    slot_reals = 2 * slot_count
    first_slot = (lax.axis_index("lat") * lon_count + lax.axis_index("lon")) * slot_count
    held_waves = lax.dynamic_slice_in_dim(wave_ids, first_slot, slot_count)
    degree_ids = jnp.arange(degree_count, dtype=jnp.int32)
    masked = jnp.where(
        degree_ids[None, None, :] >= held_waves[:, None, None],
        legendre,
        jnp.zeros((), legendre.dtype),
    )
    forward_table, inverse_table = build_tables(wave_ids)

    def analyze(source, twiddle):
        spectra = jnp.einsum(
            "srnc,kn->srkc", source, twiddle, preferred_element_type=jnp.float32
        ).astype(jnp.bfloat16)
        gathered = lax.all_to_all(spectra, ("lat", "lon"), split_axis=2, concat_axis=1, tiled=True)
        blocks = gathered.reshape(samples, lat_cells, slot_count, 2 * channels)
        spectral = jnp.einsum("samc,mal->slmc", blocks, masked, preferred_element_type=jnp.float32)
        peers = lat_count * lon_count
        spectral = spectral.astype(jnp.bfloat16).reshape(
            peers, degree_count // peers, slot_count, 2 * channels
        )
        return lax.all_to_all(spectral, ("lat", "lon"), split_axis=0, concat_axis=0, tiled=True)

    def synthesize(spectral, twiddle):
        joined = lax.all_to_all(spectral, ("lat", "lon"), split_axis=0, concat_axis=0, tiled=True)
        blocks = joined.reshape(samples, degree_count, slot_count, 2 * channels)
        spectra = jnp.einsum(
            "slmc,mal->samc", blocks, masked, preferred_element_type=jnp.float32
        ).astype(jnp.bfloat16)
        spectra = spectra.reshape(samples, lat_cells, slot_reals, channels)
        pencil = lax.all_to_all(spectra, ("lat", "lon"), split_axis=1, concat_axis=2, tiled=True)
        return jnp.einsum("srkc,kn->srnc", pencil, twiddle, preferred_element_type=jnp.float32)

    coef_rows = analyze(state_grid, forward_table)
    held_count = weights.shape[0] // lon_count
    held_weights = lax.dynamic_slice_in_dim(weights, lax.axis_index("lon") * held_count, held_count)
    real_bd, imag_bd = block_diagonal(held_weights)
    mixing = jnp.concatenate(
        [
            jnp.concatenate([real_bd, imag_bd], axis=2),
            jnp.concatenate([-imag_bd, real_bd], axis=2),
        ],
        axis=1,
    )
    mixed_rows = jnp.einsum(
        "slmc,lcd->slmd", coef_rows, mixing, preferred_element_type=jnp.float32
    ).astype(jnp.bfloat16)
    branch = synthesize(mixed_rows, inverse_table)
    pulled = (cotangent.astype(jnp.float32) * gelu_slope(branch)).astype(jnp.bfloat16)
    back_rows = analyze(pulled, inverse_table)
    pair_products = jnp.einsum(
        "slmc,slmd->lcd", coef_rows, back_rows, preferred_element_type=jnp.float32
    )
    width = GROUPS * GROUP_WIDTH
    same_part = pair_products[:, :width, :width] + pair_products[:, width:, width:]
    cross_part = pair_products[:, :width, width:] - pair_products[:, width:, :width]
    grad_full = jnp.concatenate([same_part, cross_part], axis=2)
    rows_group = lax.broadcasted_iota(jnp.int32, (width, 2 * width), 0) // GROUP_WIDTH
    cols_group = lax.broadcasted_iota(jnp.int32, (width, 2 * width), 1) % width // GROUP_WIDTH
    grad_terms = jnp.where(
        rows_group == cols_group, grad_full.astype(jnp.bfloat16), jnp.zeros((), jnp.bfloat16)
    )
    pick_in = lax.broadcasted_iota(jnp.int32, (2 * width, 2 * GROUP_WIDTH), 0)
    pick_out = lax.broadcasted_iota(jnp.int32, (2 * width, 2 * GROUP_WIDTH), 1)
    picker = (
        (pick_in // width == pick_out // GROUP_WIDTH)
        & (pick_in % GROUP_WIDTH == pick_out % GROUP_WIDTH)
    ).astype(jnp.bfloat16)
    compact = jnp.einsum("lcd,de->lce", grad_terms, picker, preferred_element_type=jnp.float32)
    local_grad = (
        compact.reshape(held_count, GROUPS, GROUP_WIDTH, 2, GROUP_WIDTH)
        .transpose(0, 3, 1, 2, 4)
        .reshape(held_weights.shape)
    )
    weight_grad = gather_sum(local_grad.astype(jnp.bfloat16), "dp", ("lon", "dp"))
    weight_grad = weight_grad.reshape(weights.shape).astype(jnp.float32)
    demixed_rows = jnp.einsum(
        "slmd,lcd->slmc", back_rows, mixing, preferred_element_type=jnp.float32
    ).astype(jnp.bfloat16)
    returned = synthesize(demixed_rows, forward_table)
    input_grad = (cotangent.astype(jnp.float32) + returned).astype(jnp.bfloat16)
    return (input_grad, weight_grad)


def solution(mesh):
    return jax.shard_map(
        shards,
        mesh=mesh,
        in_specs=(
            P("dp", ("lat", "lon"), None, None),
            P("dp", ("lat", "lon"), None, None),
            P(("lat", "lon"), None, None),
            P(),
            P("lat", None, None, None),
        ),
        out_specs=(P("dp", ("lat", "lon"), None, None), P("lat", None, None, None)),
        check_vma=False,
    )
```
